512 devices in a mesh: dp: 32 (over z, x), fsdp: 16 (over y, core).
Axes of the slice: x: 4, y: 8, z: 8, core: 2. Of those that a mesh axis runs over, the one named last changes fastest.
Arguments:
- projected: bfloat16 [65536, 2304], P(('dp', 'fsdp')), may hold values from -7.03125 to 7.03125
- out_weight: bfloat16 [768, 1536], P('fsdp'), may hold values from -0.21875 to 0.21875
- kernel: float32 [31, 1536], replicated, may hold values from -2 to 2
- cotangent: bfloat16 [65536, 1536], P(('dp', 'fsdp')), may hold values from -6 to 6
- send_rows: int32 [65536], P(('dp', 'fsdp')), may hold values from -1 to 127, as said below
- compute_src: int32 [65536], P(('dp', 'fsdp')), may hold values from -1 to 127, as said below
- segment: int32 [65536], P(('dp', 'fsdp')), may hold values from -1 to 3, as said below
Outputs:
- block_out: bfloat16 [65536, 1536], P(('dp', 'fsdp'))
- projected_grad: bfloat16 [65536, 2304], P(('dp', 'fsdp'))
- out_weight_grad: float32 [768, 1536], P('fsdp')
- kernel_grad: float32 [31, 1536], replicated
The draws below stay inside these ranges and needn't reach their ends.
Inputs may be any that keep to these rules, and one draw needn't show every extreme that they name: `send_rows`: A device's 128 entries are 32 blocks of 4, block t for index t of dp at the same fsdp index; each lists rows of the device's own block of projected, each row at most once, filled entries first in a block and -1 after them. In every draw some device of each fsdp index fills all its entries. `compute_src`: on device (t, f), a row holds s * 4 + k when it receives entry t * 4 + k of device (s, f); every filled entry of send_rows is received by exactly one row, and a row holds -1 when it receives nothing. Filled rows come first. In every draw some device of each fsdp index receives a full block from every device. On each device, rows with compute_src = -1 hold -1, the others hold segment numbers from 0 that never fall along the rows.
All inputs are finite; a program needn't handle non-finite values.
Results may differ from the reference program's by a relative error of at most 0.018.
Values may be sent and summed in bfloat16 or wider, within the bound.
No kernel may reach another device: no remote copies, remote signals or barrier semaphores. Data moves between devices by JAX's collectives and lax.ppermute only.
A program may use at most 128 MiB of HBM per device.

```python
import jax
import jax.numpy as jnp
from jax import lax

D_MODEL = 1536
HEADS = 8
HEAD_DIM = 96
KERNEL = 31
ROWS = 128
SLOTS = 4
TOKENS = 65536
N_DP = 32
N_FSDP = 16


def packing_plan(key):
    base_key = jax.random.fold_in(key, 4099)
    level_key, forced_key, target_key, share_key, order_key, split_key = jax.random.split(base_key, 6)
    levels = jax.random.randint(level_key, (N_DP, N_FSDP), 1, SLOTS + 1)
    forced = jax.random.randint(forced_key, (N_FSDP,), 0, N_DP)
    busiest = jnp.arange(N_DP)[:, None] == forced[None, :]
    levels = jnp.where(busiest, SLOTS, levels)
    lowest = levels // 2
    spread = levels - lowest + 1
    raw_draw = jax.random.randint(share_key, (N_DP, N_FSDP, N_DP), 0, 1 << 20)
    shares = lowest[..., None] + raw_draw % spread[..., None]
    full_target = jax.random.randint(target_key, (N_FSDP,), 0, N_DP)
    to_full = jnp.arange(N_DP)[None, None, :] == full_target[None, :, None]
    shares = jnp.where(busiest[..., None] | to_full, SLOTS, shares)
    order_keys = jax.random.split(order_key, N_DP * N_FSDP)
    orders = jax.vmap(lambda one_key: jax.random.permutation(one_key, ROWS))(order_keys).reshape(N_DP, N_FSDP, ROWS).astype(jnp.int32)
    slot_k = jnp.arange(SLOTS)
    before = jnp.cumsum(shares, axis=2) - shares
    item_index = jnp.minimum(before[..., None] + slot_k, ROWS - 1)
    used_slot = slot_k < shares[..., None]
    listed = jnp.take_along_axis(orders, item_index.reshape(N_DP, N_FSDP, ROWS), axis=2)
    send_rows = jnp.where(used_slot.reshape(N_DP, N_FSDP, ROWS), listed, -1).astype(jnp.int32)
    earlier = jnp.cumsum(shares, axis=0) - shares
    position = jnp.where(used_slot, earlier[..., None] + slot_k, ROWS)
    source_code = jnp.broadcast_to(jnp.arange(N_DP)[:, None, None, None] * SLOTS + slot_k, position.shape)
    target_axis = jnp.broadcast_to(jnp.arange(N_DP)[None, None, :, None], position.shape)
    column_axis = jnp.broadcast_to(jnp.arange(N_FSDP)[None, :, None, None], position.shape)
    compute_src = jnp.full((N_DP, N_FSDP, ROWS + 1), -1, jnp.int32).at[target_axis, column_axis, position].set(source_code.astype(jnp.int32))[..., :ROWS]
    totals = jnp.sum(shares, axis=0).T
    row_ids = jnp.arange(ROWS)
    breaks = jax.random.randint(split_key, (N_DP, N_FSDP, ROWS), 0, 40) == 0
    starts = breaks | (row_ids % (ROWS // 4) == 0)
    numbered = jnp.minimum(jnp.cumsum(starts.astype(jnp.int32), axis=2) - 1, 3)
    segment = jnp.where(row_ids < totals[..., None], numbered, -1).astype(jnp.int32)
    return (send_rows, compute_src, segment)


def draw_send_rows(key, part):
    return packing_plan(key)[0].reshape(-1)


def draw_compute_src(key, part):
    return packing_plan(key)[1].reshape(-1)


def draw_segment(key, part):
    return packing_plan(key)[2].reshape(-1)


def draw_projected(key, part):
    inner_width = HEADS * HEAD_DIM
    noise_key = jax.random.fold_in(jax.random.fold_in(key, 77), 0)
    noise_field = jnp.clip(jax.random.normal(noise_key, (TOKENS, 3 * inner_width), jnp.float32), -4.0, 4.0)
    return noise_field.astype(jnp.bfloat16)


def steps_of(key, extent, cuts, smallest, high):
    loudness, own = 1.0, jax.random.fold_in(key, 6)
    for axis_at, blocks in cuts:
        steps = jnp.exp(jax.random.uniform(jax.random.fold_in(own, axis_at), (blocks,), jnp.float32, smallest / len(cuts), high / len(cuts)))
        loudness = loudness * jnp.repeat(steps, extent[axis_at] // blocks).reshape([-1 if axis == axis_at else 1 for axis in range(len(extent))])
    return loudness


def noise(rng, extent, width, most, cuts=(), kind=jnp.bfloat16):
    values = jax.random.normal(rng, extent, jnp.float32) * width
    if len(cuts) > 0:
        values = steps_of(rng, extent, cuts, -0.22, 0.18) * values
    return jnp.clip(values, min=-most, max=most).astype(kind)


def setup_inputs(seed: int = 0) -> dict:
    key_list = jax.random.split(jax.random.key(seed), 8)
    return {
        "projected": draw_projected(jax.random.fold_in(key_list[7], 71), 0),
        "out_weight": noise(key_list[1], (HEADS * HEAD_DIM, D_MODEL), (HEADS * HEAD_DIM) ** -0.5, 0.21875, ((0, 16),)),
        "kernel": noise(key_list[2], (KERNEL, D_MODEL), 8 ** -0.5, 2.0, (), jnp.float32),
        "cotangent": noise(key_list[3], (TOKENS, D_MODEL), 1.0, 6.0, ((0, 512),)),
        "send_rows": draw_send_rows(jax.random.fold_in(key_list[7], 71), 0),
        "compute_src": draw_compute_src(jax.random.fold_in(key_list[7], 71), 0),
        "segment": draw_segment(jax.random.fold_in(key_list[7], 71), 0),
    }


def split_heads(frames):
    length = frames.shape[0]
    inner_width = HEADS * HEAD_DIM
    query_part = frames[:, :inner_width].reshape(length, HEADS, HEAD_DIM)
    key_part = frames[:, inner_width:2 * inner_width].reshape(length, HEADS, HEAD_DIM)
    value_part = frames[:, 2 * inner_width:].reshape(length, HEADS, HEAD_DIM)
    return (query_part, key_part, value_part)

def attend(frames, segment):
    query_part, key_part, value_part = split_heads(frames)
    scores = jnp.einsum('qhd,khd->hqk', query_part.astype(jnp.float32), key_part.astype(jnp.float32)) * HEAD_DIM ** (-0.5)
    inside = segment[:, None] == segment[None, :]
    scores = jnp.where(inside[None], scores, -1e+30)
    highest = lax.optimization_barrier(jnp.max(scores, axis=2, keepdims=True))
    weights = jnp.exp(scores - highest)
    soft_probs = weights / lax.optimization_barrier(jnp.sum(weights, axis=2, keepdims=True))
    rounded = soft_probs.astype(jnp.bfloat16)
    context = jnp.einsum('hqk,khd->qhd', rounded.astype(jnp.float32), value_part.astype(jnp.float32))
    return (context.reshape(frames.shape[0], HEADS * HEAD_DIM).astype(jnp.bfloat16), soft_probs, rounded)

def attend_back(frames, soft_probs, rounded, context_grad):
    query_part, key_part, value_part = split_heads(frames)
    length = frames.shape[0]
    inner_width = HEADS * HEAD_DIM
    upstream = context_grad.reshape(length, HEADS, HEAD_DIM).astype(jnp.float32)
    value_grad = jnp.einsum('hqk,qhd->khd', rounded.astype(jnp.float32), upstream)
    prob_grad = jnp.einsum('qhd,khd->hqk', upstream, value_part.astype(jnp.float32))
    score_grad = soft_probs * (prob_grad - lax.optimization_barrier(jnp.sum(prob_grad * soft_probs, axis=2, keepdims=True)))
    score_grad = (score_grad * HEAD_DIM ** (-0.5)).astype(jnp.bfloat16).astype(jnp.float32)
    query_grad = jnp.einsum('hqk,khd->qhd', score_grad, key_part.astype(jnp.float32))
    key_grad = jnp.einsum('hqk,qhd->khd', score_grad, query_part.astype(jnp.float32))
    return jnp.concatenate([query_grad.reshape(length, inner_width).astype(jnp.bfloat16), key_grad.reshape(length, inner_width).astype(jnp.bfloat16), value_grad.reshape(length, inner_width).astype(jnp.bfloat16)], axis=1)

def finish(mixed, kernel, segment):
    length = mixed.shape[0]
    tap_count = kernel.shape[0]
    half_span = (tap_count - 1) // 2
    signal = mixed.astype(jnp.float32)
    padded = jnp.pad(signal, ((half_span, half_span), (0, 0)))
    neighbours = jnp.pad(segment, (half_span, half_span), constant_values=-2)
    convolved = jnp.zeros_like(signal)
    for offset in range(tap_count):
        matching = (neighbours[offset:offset + length] == segment).astype(jnp.float32)
        convolved = convolved + kernel[offset] * padded[offset:offset + length] * matching[:, None]
    return signal + jax.nn.silu(convolved)

def place_rows(target_index, values):
    clamped = jnp.where(target_index >= 0, target_index, ROWS)
    return jnp.zeros((ROWS, values.shape[1]), values.dtype).at[clamped].set(values, mode='drop')

def reference(projected, out_weight, kernel, cotangent, send_rows, compute_src, segment):
    devices = N_DP * N_FSDP
    width_all = projected.shape[1]
    arrival = projected.reshape(N_DP, N_FSDP, ROWS, width_all)
    slot_rows = send_rows.reshape(N_DP, N_FSDP, ROWS)
    present = slot_rows >= 0
    picked = jnp.take_along_axis(arrival, jnp.maximum(slot_rows, 0)[..., None], axis=2)
    picked = jnp.where(present[..., None], picked, jnp.zeros_like(picked))
    incoming = picked.reshape(N_DP, N_FSDP, N_DP, SLOTS, width_all).transpose(2, 1, 0, 3, 4).reshape(devices, ROWS, width_all)
    sources = compute_src.reshape(devices, ROWS)
    filled = sources >= 0
    frames = jnp.take_along_axis(incoming, jnp.maximum(sources, 0)[..., None], axis=1)
    frames = jnp.where(filled[..., None], frames, jnp.zeros_like(frames))
    segments_all = segment.reshape(devices, ROWS)
    upstream = cotangent.reshape(devices, ROWS, D_MODEL)

    def one_device(running, inputs_one):
        frame_rows, seg_rows, cot_rows = inputs_one
        context, soft_probs, rounded = attend(frame_rows, seg_rows)
        mixed = jnp.dot(context, out_weight, preferred_element_type=jnp.float32).astype(jnp.bfloat16)
        result, pullback = jax.vjp(lambda signal, kernel_taps: finish(signal, kernel_taps, seg_rows), mixed, kernel)
        mixed_grad, kernel_part = pullback(cot_rows.astype(jnp.float32))
        weight_part = jnp.dot(context.T, mixed_grad, preferred_element_type=jnp.float32).astype(jnp.bfloat16)
        weight_part = lax.optimization_barrier(weight_part).astype(jnp.float32)
        context_grad = jnp.dot(mixed_grad, out_weight.T, preferred_element_type=jnp.float32).astype(jnp.bfloat16)
        frame_grad = attend_back(frame_rows, soft_probs, rounded, context_grad)
        return ((running[0] + weight_part, running[1] + kernel_part), (result.astype(jnp.bfloat16), frame_grad))
    zero_sums = (jnp.zeros(out_weight.shape, jnp.float32), jnp.zeros(kernel.shape, jnp.float32))
    (weight_sum, kernel_sum), (outputs, frame_grads) = lax.scan(one_device, zero_sums, (frames, segments_all, upstream))
    returning = jax.vmap(place_rows)(sources, frame_grads)
    returning = returning.reshape(N_DP, N_FSDP, N_DP, SLOTS, width_all).transpose(2, 1, 0, 3, 4).reshape(devices, ROWS, width_all)
    projected_grad = jax.vmap(place_rows)(slot_rows.reshape(devices, ROWS), returning)
    scale_factor = TOKENS ** (-0.5)
    return (outputs.reshape(TOKENS, D_MODEL), projected_grad.reshape(TOKENS, width_all), weight_sum * scale_factor, kernel_sum * scale_factor)
```

```python
import jax
import jax.numpy as jnp
from jax import lax
from jax.sharding import PartitionSpec as P

HEADS = 8
HEAD_DIM = 96


def split_heads(frames):
    length = frames.shape[0]
    inner_width = HEADS * HEAD_DIM
    query_part = frames[:, :inner_width].reshape(length, HEADS, HEAD_DIM)
    key_part = frames[:, inner_width : 2 * inner_width].reshape(length, HEADS, HEAD_DIM)
    value_part = frames[:, 2 * inner_width :].reshape(length, HEADS, HEAD_DIM)
    return (query_part, key_part, value_part)


def attend(frames, segment):
    query_part, key_part, value_part = split_heads(frames)
    scores = jnp.einsum(
        "qhd,khd->hqk", query_part, key_part, preferred_element_type=jnp.float32
    ) * HEAD_DIM ** (-0.5)
    inside = segment[:, None] == segment[None, :]
    scores = jnp.where(inside[None], scores, -1e30)
    highest = jnp.max(scores, axis=2, keepdims=True)
    weights = jnp.exp(scores - highest)
    soft_probs = weights / jnp.sum(weights, axis=2, keepdims=True)
    rounded = soft_probs.astype(jnp.bfloat16)
    context = jnp.einsum("hqk,khd->qhd", rounded, value_part, preferred_element_type=jnp.float32)
    return (
        context.reshape(frames.shape[0], HEADS * HEAD_DIM).astype(jnp.bfloat16),
        soft_probs,
        rounded,
    )


def attend_back(frames, soft_probs, rounded, context_grad):
    query_part, key_part, value_part = split_heads(frames)
    length = frames.shape[0]
    inner_width = HEADS * HEAD_DIM
    upstream = context_grad.reshape(length, HEADS, HEAD_DIM)
    value_grad = jnp.einsum("hqk,qhd->khd", rounded, upstream, preferred_element_type=jnp.float32)
    prob_grad = jnp.einsum("qhd,khd->hqk", upstream, value_part, preferred_element_type=jnp.float32)
    score_grad = soft_probs * (prob_grad - jnp.sum(prob_grad * soft_probs, axis=2, keepdims=True))
    score_grad = (score_grad * HEAD_DIM ** (-0.5)).astype(jnp.bfloat16)
    query_grad = jnp.einsum(
        "hqk,khd->qhd", score_grad, key_part, preferred_element_type=jnp.float32
    )
    key_grad = jnp.einsum(
        "hqk,qhd->khd", score_grad, query_part, preferred_element_type=jnp.float32
    )
    return jnp.concatenate(
        [
            query_grad.reshape(length, inner_width).astype(jnp.bfloat16),
            key_grad.reshape(length, inner_width).astype(jnp.bfloat16),
            value_grad.reshape(length, inner_width).astype(jnp.bfloat16),
        ],
        axis=1,
    )


def finish(mixed, kernel, segment):
    length = mixed.shape[0]
    tap_count = kernel.shape[0]
    half_span = (tap_count - 1) // 2
    signal = mixed.astype(jnp.float32)
    padded = jnp.pad(signal, ((half_span, half_span), (0, 0)))
    neighbours = jnp.pad(segment, (half_span, half_span), constant_values=-2)
    convolved = jnp.zeros_like(signal)
    for offset in range(tap_count):
        matching = (neighbours[offset : offset + length] == segment).astype(jnp.float32)
        convolved = (
            convolved + kernel[offset] * padded[offset : offset + length] * matching[:, None]
        )
    return signal + jax.nn.silu(convolved)


def body(projected, out_weight, kernel, cotangent, send_rows, compute_src, segment):
    row_count = projected.shape[0]
    present = send_rows >= 0
    outgoing = jnp.take(projected, jnp.maximum(send_rows, 0), axis=0)
    outgoing = jnp.where(present[:, None], outgoing, jnp.zeros_like(outgoing))
    incoming = lax.all_to_all(outgoing, "dp", split_axis=0, concat_axis=0, tiled=True)
    filled = compute_src >= 0
    frames = jnp.take(incoming, jnp.maximum(compute_src, 0), axis=0)
    frames = jnp.where(filled[:, None], frames, jnp.zeros_like(frames))
    context, soft_probs, rounded = attend(frames, segment)
    columns = context
    mixed_sums = jnp.dot(
        columns,
        lax.all_gather(out_weight, "fsdp", axis=0, tiled=True),
        preferred_element_type=jnp.float32,
    )
    mixed = mixed_sums.astype(jnp.bfloat16)
    result, pullback = jax.vjp(
        lambda signal, kernel_taps: finish(signal, kernel_taps, segment), mixed, kernel
    )
    mixed_grad, kernel_part = pullback(cotangent.astype(jnp.float32))
    columns = context
    weight_share = lax.psum_scatter(
        jnp.einsum("rc,rd->cd", columns, mixed_grad, preferred_element_type=jnp.float32).astype(
            jnp.bfloat16
        ),
        "fsdp",
        scatter_dimension=0,
        tiled=True,
    ).astype(jnp.float32)
    context_grad = jnp.einsum(
        "rd,cd->rc",
        mixed_grad,
        lax.all_gather(out_weight, "fsdp", axis=0, tiled=True),
        preferred_element_type=jnp.float32,
    ).astype(jnp.bfloat16)
    frame_grad = attend_back(frames, soft_probs, rounded, context_grad)
    slot_total = incoming.shape[0]
    back_index = jnp.where(filled, compute_src, slot_total)
    returning = jnp.zeros_like(incoming).at[back_index].set(frame_grad, mode="drop")
    arrived = lax.all_to_all(returning, "dp", split_axis=0, concat_axis=0, tiled=True)
    source_index = jnp.where(present, send_rows, row_count)
    projected_grad = jnp.zeros_like(projected).at[source_index].set(arrived, mode="drop")
    scale_factor = (row_count * lax.axis_size("dp") * lax.axis_size("fsdp")) ** (-0.5)
    kernel_f = lax.psum(kernel_part, "fsdp")
    both = dp_allreduce_a2a(jnp.concatenate([weight_share, kernel_f, jnp.zeros((17, 1536), jnp.float32)], axis=0))
    weight_total, kernel_total = both[:48], both[48:79]
    return (
        result.astype(jnp.bfloat16),
        projected_grad,
        weight_total * scale_factor,
        kernel_total * scale_factor,
    )


def dp_allreduce_rs_ag(x):
    n = lax.axis_size("dp")
    flat = x.reshape(n, -1)
    part = lax.psum_scatter(flat, "dp", scatter_dimension=0, tiled=True)
    return lax.all_gather(part, "dp", axis=0, tiled=True).reshape(x.shape)


def dp_allreduce_a2a(x):
    n = lax.axis_size("dp")
    flat = x.reshape(n, -1)
    got = lax.all_to_all(flat, "dp", split_axis=0, concat_axis=0, tiled=True)
    part = jnp.sum(got, axis=0, keepdims=True)
    return lax.all_gather(part, "dp", axis=0, tiled=True).reshape(x.shape)


def dp_allreduce_a2a2(x):
    n = lax.axis_size("dp")
    flat = x.reshape(n, -1)
    got = lax.all_to_all(flat, "dp", split_axis=0, concat_axis=0, tiled=True)
    part = jnp.sum(got, axis=0, keepdims=True)
    back = lax.all_to_all(jnp.broadcast_to(part, flat.shape), "dp", split_axis=0, concat_axis=0, tiled=True)
    return back.reshape(x.shape)


def solution(mesh):
    placed = (
        P(("dp", "fsdp"), None),
        P("fsdp", None),
        P(),
        P(("dp", "fsdp"), None),
        P(("dp", "fsdp")),
        P(("dp", "fsdp")),
        P(("dp", "fsdp")),
    )
    return jax.shard_map(
        body,
        mesh=mesh,
        in_specs=placed,
        out_specs=(P(("dp", "fsdp"), None), P(("dp", "fsdp"), None), P("fsdp", None), P()),
        check_vma=False,
    )
```

```python
import jax
import jax.numpy as jnp
from jax import lax
from jax.sharding import PartitionSpec as P

HEADS = 8
HEAD_DIM = 96


def split_heads(frames):
    length = frames.shape[0]
    inner_width = HEADS * HEAD_DIM
    query_part = frames[:, :inner_width].reshape(length, HEADS, HEAD_DIM)
    key_part = frames[:, inner_width : 2 * inner_width].reshape(length, HEADS, HEAD_DIM)
    value_part = frames[:, 2 * inner_width :].reshape(length, HEADS, HEAD_DIM)
    return (query_part, key_part, value_part)


def attend(frames, segment):
    query_part, key_part, value_part = split_heads(frames)
    scores = jnp.einsum(
        "qhd,khd->hqk", query_part, key_part, preferred_element_type=jnp.float32
    ) * HEAD_DIM ** (-0.5)
    inside = segment[:, None] == segment[None, :]
    scores = jnp.where(inside[None], scores, -1e30)
    highest = jnp.max(scores, axis=2, keepdims=True)
    weights = jnp.exp(scores - highest)
    soft_probs = weights / jnp.sum(weights, axis=2, keepdims=True)
    rounded = soft_probs.astype(jnp.bfloat16)
    context = jnp.einsum("hqk,khd->qhd", rounded, value_part, preferred_element_type=jnp.float32)
    return (
        context.reshape(frames.shape[0], HEADS * HEAD_DIM).astype(jnp.bfloat16),
        soft_probs,
        rounded,
    )


def attend_back(frames, soft_probs, rounded, context_grad):
    query_part, key_part, value_part = split_heads(frames)
    length = frames.shape[0]
    inner_width = HEADS * HEAD_DIM
    upstream = context_grad.reshape(length, HEADS, HEAD_DIM)
    value_grad = jnp.einsum("hqk,qhd->khd", rounded, upstream, preferred_element_type=jnp.float32)
    prob_grad = jnp.einsum("qhd,khd->hqk", upstream, value_part, preferred_element_type=jnp.float32)
    score_grad = soft_probs * (prob_grad - jnp.sum(prob_grad * soft_probs, axis=2, keepdims=True))
    score_grad = (score_grad * HEAD_DIM ** (-0.5)).astype(jnp.bfloat16)
    query_grad = jnp.einsum(
        "hqk,khd->qhd", score_grad, key_part, preferred_element_type=jnp.float32
    )
    key_grad = jnp.einsum(
        "hqk,qhd->khd", score_grad, query_part, preferred_element_type=jnp.float32
    )
    return jnp.concatenate(
        [
            query_grad.reshape(length, inner_width).astype(jnp.bfloat16),
            key_grad.reshape(length, inner_width).astype(jnp.bfloat16),
            value_grad.reshape(length, inner_width).astype(jnp.bfloat16),
        ],
        axis=1,
    )


def finish(mixed, kernel, segment):
    length = mixed.shape[0]
    tap_count = kernel.shape[0]
    half_span = (tap_count - 1) // 2
    signal = mixed.astype(jnp.float32)
    padded = jnp.pad(signal, ((half_span, half_span), (0, 0)))
    neighbours = jnp.pad(segment, (half_span, half_span), constant_values=-2)
    convolved = jnp.zeros_like(signal)
    for offset in range(tap_count):
        matching = (neighbours[offset : offset + length] == segment).astype(jnp.float32)
        convolved = (
            convolved + kernel[offset] * padded[offset : offset + length] * matching[:, None]
        )
    return signal + jax.nn.silu(convolved)


def body(projected, out_weight, kernel, cotangent, send_rows, compute_src, segment):
    row_count = projected.shape[0]
    present = send_rows >= 0
    outgoing = jnp.take(projected, jnp.maximum(send_rows, 0), axis=0)
    outgoing = jnp.where(present[:, None], outgoing, jnp.zeros_like(outgoing))
    incoming = lax.all_to_all(outgoing, "dp", split_axis=0, concat_axis=0, tiled=True)
    filled = compute_src >= 0
    frames = jnp.take(incoming, jnp.maximum(compute_src, 0), axis=0)
    frames = jnp.where(filled[:, None], frames, jnp.zeros_like(frames))
    context, soft_probs, rounded = attend(frames, segment)
    columns = context
    mixed_sums = jnp.dot(
        columns,
        lax.all_gather(out_weight, "fsdp", axis=0, tiled=True),
        preferred_element_type=jnp.float32,
    )
    mixed = mixed_sums.astype(jnp.bfloat16)
    result, pullback = jax.vjp(
        lambda signal, kernel_taps: finish(signal, kernel_taps, segment), mixed, kernel
    )
    mixed_grad, kernel_part = pullback(cotangent.astype(jnp.float32))
    columns = context
    weight_share = lax.psum_scatter(
        jnp.einsum("rc,rd->cd", columns, mixed_grad, preferred_element_type=jnp.float32).astype(
            jnp.bfloat16
        ),
        "fsdp",
        scatter_dimension=0,
        tiled=True,
    ).astype(jnp.float32)
    context_grad = jnp.einsum(
        "rd,cd->rc",
        mixed_grad,
        lax.all_gather(out_weight, "fsdp", axis=0, tiled=True),
        preferred_element_type=jnp.float32,
    ).astype(jnp.bfloat16)
    frame_grad = attend_back(frames, soft_probs, rounded, context_grad)
    slot_total = incoming.shape[0]
    back_index = jnp.where(filled, compute_src, slot_total)
    returning = jnp.zeros_like(incoming).at[back_index].set(frame_grad, mode="drop")
    arrived = lax.all_to_all(returning, "dp", split_axis=0, concat_axis=0, tiled=True)
    source_index = jnp.where(present, send_rows, row_count)
    projected_grad = jnp.zeros_like(projected).at[source_index].set(arrived, mode="drop")
    scale_factor = (row_count * lax.axis_size("dp") * lax.axis_size("fsdp")) ** (-0.5)
    kernel_piece = fsdp_sum_rows(kernel_part)
    owned_rows = weight_share.shape[0]
    both = dp_allreduce_a2a(jnp.concatenate([weight_share, kernel_piece], axis=0))
    weight_total = both[:owned_rows]
    kernel_total = lax.all_gather(both[owned_rows:], "fsdp", axis=0, tiled=True)[: kernel.shape[0]]
    return (
        result.astype(jnp.bfloat16),
        projected_grad,
        weight_total * scale_factor,
        kernel_total * scale_factor,
    )


def fsdp_sum_rows(x):
    n = lax.axis_size("fsdp")
    per = -(-x.shape[0] // n)
    padded = jnp.pad(x, ((0, n * per - x.shape[0]), (0, 0)))
    got = lax.all_to_all(padded.reshape(n, per, x.shape[1]), "fsdp", split_axis=0, concat_axis=0, tiled=True)
    return jnp.sum(got, axis=0)


def dp_allreduce_a2a(x):
    n = lax.axis_size("dp")
    per = -(-x.shape[0] // n)
    padded = jnp.pad(x, ((0, n * per - x.shape[0]), (0, 0))).reshape(n, per, x.shape[1])
    got = lax.all_to_all(padded, "dp", split_axis=0, concat_axis=0, tiled=True)
    part = jnp.sum(got, axis=0, keepdims=True)
    whole = lax.all_gather(part, "dp", axis=0, tiled=True)
    return whole.reshape(n * per, x.shape[1])[: x.shape[0]]

def solution(mesh):
    placed = (
        P(("dp", "fsdp"), None),
        P("fsdp", None),
        P(),
        P(("dp", "fsdp"), None),
        P(("dp", "fsdp")),
        P(("dp", "fsdp")),
        P(("dp", "fsdp")),
    )
    return jax.shard_map(
        body,
        mesh=mesh,
        in_specs=placed,
        out_specs=(P(("dp", "fsdp"), None), P(("dp", "fsdp"), None), P("fsdp", None), P()),
        check_vma=False,
    )
```

```python
import jax
import jax.numpy as jnp
from jax import lax
from jax.sharding import PartitionSpec as P

HEADS = 8
HEAD_DIM = 96


def split_heads(frames):
    length = frames.shape[0]
    inner_width = HEADS * HEAD_DIM
    query_part = frames[:, :inner_width].reshape(length, HEADS, HEAD_DIM)
    key_part = frames[:, inner_width : 2 * inner_width].reshape(length, HEADS, HEAD_DIM)
    value_part = frames[:, 2 * inner_width :].reshape(length, HEADS, HEAD_DIM)
    return (query_part, key_part, value_part)


def attend(frames, segment):
    query_part, key_part, value_part = split_heads(frames)
    scores = jnp.einsum(
        "qhd,khd->hqk", query_part, key_part, preferred_element_type=jnp.float32
    ) * HEAD_DIM ** (-0.5)
    inside = segment[:, None] == segment[None, :]
    scores = jnp.where(inside[None], scores, -1e30)
    highest = jnp.max(scores, axis=2, keepdims=True)
    weights = jnp.exp(scores - highest)
    soft_probs = weights / jnp.sum(weights, axis=2, keepdims=True)
    rounded = soft_probs.astype(jnp.bfloat16)
    context = jnp.einsum("hqk,khd->qhd", rounded, value_part, preferred_element_type=jnp.float32)
    return (
        context.reshape(frames.shape[0], HEADS * HEAD_DIM).astype(jnp.bfloat16),
        soft_probs,
        rounded,
    )


def attend_back(frames, soft_probs, rounded, context_grad):
    query_part, key_part, value_part = split_heads(frames)
    length = frames.shape[0]
    inner_width = HEADS * HEAD_DIM
    upstream = context_grad.reshape(length, HEADS, HEAD_DIM)
    value_grad = jnp.einsum("hqk,qhd->khd", rounded, upstream, preferred_element_type=jnp.float32)
    prob_grad = jnp.einsum("qhd,khd->hqk", upstream, value_part, preferred_element_type=jnp.float32)
    score_grad = soft_probs * (prob_grad - jnp.sum(prob_grad * soft_probs, axis=2, keepdims=True))
    score_grad = (score_grad * HEAD_DIM ** (-0.5)).astype(jnp.bfloat16)
    query_grad = jnp.einsum(
        "hqk,khd->qhd", score_grad, key_part, preferred_element_type=jnp.float32
    )
    key_grad = jnp.einsum(
        "hqk,qhd->khd", score_grad, query_part, preferred_element_type=jnp.float32
    )
    return jnp.concatenate(
        [
            query_grad.reshape(length, inner_width).astype(jnp.bfloat16),
            key_grad.reshape(length, inner_width).astype(jnp.bfloat16),
            value_grad.reshape(length, inner_width).astype(jnp.bfloat16),
        ],
        axis=1,
    )


def finish(mixed, kernel, segment):
    length = mixed.shape[0]
    tap_count = kernel.shape[0]
    half_span = (tap_count - 1) // 2
    signal = mixed.astype(jnp.float32)
    padded = jnp.pad(signal, ((half_span, half_span), (0, 0)))
    neighbours = jnp.pad(segment, (half_span, half_span), constant_values=-2)
    convolved = jnp.zeros_like(signal)
    for offset in range(tap_count):
        matching = (neighbours[offset : offset + length] == segment).astype(jnp.float32)
        convolved = (
            convolved + kernel[offset] * padded[offset : offset + length] * matching[:, None]
        )
    return signal + jax.nn.silu(convolved)


def body(projected, out_weight, kernel, cotangent, send_rows, compute_src, segment):
    row_count = projected.shape[0]
    present = send_rows >= 0
    outgoing = jnp.take(projected, jnp.maximum(send_rows, 0), axis=0)
    outgoing = jnp.where(present[:, None], outgoing, jnp.zeros_like(outgoing))
    incoming = lax.all_to_all(outgoing, "dp", split_axis=0, concat_axis=0, tiled=True)
    filled = compute_src >= 0
    frames = jnp.take(incoming, jnp.maximum(compute_src, 0), axis=0)
    frames = jnp.where(filled[:, None], frames, jnp.zeros_like(frames))
    context, soft_probs, rounded = attend(frames, segment)
    columns = context
    mixed_sums = jnp.dot(
        columns,
        lax.all_gather(out_weight, "fsdp", axis=0, tiled=True),
        preferred_element_type=jnp.float32,
    )
    mixed = mixed_sums.astype(jnp.bfloat16)
    result, pullback = jax.vjp(
        lambda signal, kernel_taps: finish(signal, kernel_taps, segment), mixed, kernel
    )
    mixed_grad, kernel_part = pullback(cotangent.astype(jnp.float32))
    columns = context
    weight_share = lax.psum_scatter(
        jnp.einsum("rc,rd->cd", columns, mixed_grad, preferred_element_type=jnp.float32).astype(
            jnp.bfloat16
        ),
        "fsdp",
        scatter_dimension=0,
        tiled=True,
    ).astype(jnp.float32)
    context_grad = jnp.einsum(
        "rd,cd->rc",
        mixed_grad,
        lax.all_gather(out_weight, "fsdp", axis=0, tiled=True),
        preferred_element_type=jnp.float32,
    ).astype(jnp.bfloat16)
    frame_grad = attend_back(frames, soft_probs, rounded, context_grad)
    slot_total = incoming.shape[0]
    back_index = jnp.where(filled, compute_src, slot_total)
    returning = jnp.zeros_like(incoming).at[back_index].set(frame_grad, mode="drop")
    arrived = lax.all_to_all(returning, "dp", split_axis=0, concat_axis=0, tiled=True)
    source_index = jnp.where(present, send_rows, row_count)
    projected_grad = jnp.zeros_like(projected).at[source_index].set(arrived, mode="drop")
    scale_factor = (row_count * lax.axis_size("dp") * lax.axis_size("fsdp")) ** (-0.5)
    weight_total = exchange_sum(weight_share, "dp")
    kernel_total = exchange_sum(exchange_sum(kernel_part, "fsdp"), "dp")

    return (
        result.astype(jnp.bfloat16),
        projected_grad,
        weight_total * scale_factor,
        kernel_total * scale_factor,
    )


def exchange_sum(x, axis):
    count = lax.axis_size(axis)
    assert count & (count - 1) == 0
    distance = 1
    while distance < count:
        pairs = [(index, index ^ distance) for index in range(count)]
        x = x + lax.ppermute(x, axis, pairs)
        distance *= 2
    return x


def solution(mesh):
    placed = (
        P(("dp", "fsdp"), None),
        P("fsdp", None),
        P(),
        P(("dp", "fsdp"), None),
        P(("dp", "fsdp")),
        P(("dp", "fsdp")),
        P(("dp", "fsdp")),
    )
    return jax.shard_map(
        body,
        mesh=mesh,
        in_specs=placed,
        out_specs=(P(("dp", "fsdp"), None), P(("dp", "fsdp"), None), P("fsdp", None), P()),
        check_vma=False,
    )
```

```python
import jax
import jax.numpy as jnp
from jax import lax
from jax.sharding import PartitionSpec as P

HEADS = 8
HEAD_DIM = 96


def split_heads(frames):
    length = frames.shape[0]
    inner_width = HEADS * HEAD_DIM
    query_part = frames[:, :inner_width].reshape(length, HEADS, HEAD_DIM)
    key_part = frames[:, inner_width : 2 * inner_width].reshape(length, HEADS, HEAD_DIM)
    value_part = frames[:, 2 * inner_width :].reshape(length, HEADS, HEAD_DIM)
    return (query_part, key_part, value_part)


def attend(frames, segment):
    query_part, key_part, value_part = split_heads(frames)
    scores = jnp.einsum(
        "qhd,khd->hqk", query_part, key_part, preferred_element_type=jnp.float32
    ) * HEAD_DIM ** (-0.5)
    inside = segment[:, None] == segment[None, :]
    scores = jnp.where(inside[None], scores, -1e30)
    highest = jnp.max(scores, axis=2, keepdims=True)
    weights = jnp.exp(scores - highest)
    soft_probs = weights / jnp.sum(weights, axis=2, keepdims=True)
    rounded = soft_probs.astype(jnp.bfloat16)
    context = jnp.einsum("hqk,khd->qhd", rounded, value_part, preferred_element_type=jnp.float32)
    return (
        context.reshape(frames.shape[0], HEADS * HEAD_DIM).astype(jnp.bfloat16),
        soft_probs,
        rounded,
    )


def attend_back(frames, soft_probs, rounded, context_grad):
    query_part, key_part, value_part = split_heads(frames)
    length = frames.shape[0]
    inner_width = HEADS * HEAD_DIM
    upstream = context_grad.reshape(length, HEADS, HEAD_DIM)
    value_grad = jnp.einsum("hqk,qhd->khd", rounded, upstream, preferred_element_type=jnp.float32)
    prob_grad = jnp.einsum("qhd,khd->hqk", upstream, value_part, preferred_element_type=jnp.float32)
    score_grad = soft_probs * (prob_grad - jnp.sum(prob_grad * soft_probs, axis=2, keepdims=True))
    score_grad = (score_grad * HEAD_DIM ** (-0.5)).astype(jnp.bfloat16)
    query_grad = jnp.einsum(
        "hqk,khd->qhd", score_grad, key_part, preferred_element_type=jnp.float32
    )
    key_grad = jnp.einsum(
        "hqk,qhd->khd", score_grad, query_part, preferred_element_type=jnp.float32
    )
    return jnp.concatenate(
        [
            query_grad.reshape(length, inner_width).astype(jnp.bfloat16),
            key_grad.reshape(length, inner_width).astype(jnp.bfloat16),
            value_grad.reshape(length, inner_width).astype(jnp.bfloat16),
        ],
        axis=1,
    )


def finish(mixed, kernel, segment):
    length = mixed.shape[0]
    tap_count = kernel.shape[0]
    half_span = (tap_count - 1) // 2
    signal = mixed.astype(jnp.float32)
    padded = jnp.pad(signal, ((half_span, half_span), (0, 0)))
    neighbours = jnp.pad(segment, (half_span, half_span), constant_values=-2)
    convolved = jnp.zeros_like(signal)
    for offset in range(tap_count):
        matching = (neighbours[offset : offset + length] == segment).astype(jnp.float32)
        convolved = (
            convolved + kernel[offset] * padded[offset : offset + length] * matching[:, None]
        )
    return signal + jax.nn.silu(convolved)


def body(projected, out_weight, kernel, cotangent, send_rows, compute_src, segment):
    row_count = projected.shape[0]
    present = send_rows >= 0
    outgoing = jnp.take(projected, jnp.maximum(send_rows, 0), axis=0)
    outgoing = jnp.where(present[:, None], outgoing, jnp.zeros_like(outgoing))
    incoming = lax.all_to_all(outgoing, "dp", split_axis=0, concat_axis=0, tiled=True)
    filled = compute_src >= 0
    frames = jnp.take(incoming, jnp.maximum(compute_src, 0), axis=0)
    frames = jnp.where(filled[:, None], frames, jnp.zeros_like(frames))
    context, soft_probs, rounded = attend(frames, segment)
    columns = context
    mixed_sums = jnp.dot(
        columns,
        lax.all_gather(out_weight, "fsdp", axis=0, tiled=True),
        preferred_element_type=jnp.float32,
    )
    mixed = mixed_sums.astype(jnp.bfloat16)
    result, pullback = jax.vjp(
        lambda signal, kernel_taps: finish(signal, kernel_taps, segment), mixed, kernel
    )
    mixed_grad, kernel_part = pullback(cotangent.astype(jnp.float32))
    columns = context
    weight_share = lax.psum_scatter(
        jnp.einsum("rc,rd->cd", columns, mixed_grad, preferred_element_type=jnp.float32).astype(
            jnp.bfloat16
        ),
        "fsdp",
        scatter_dimension=0,
        tiled=True,
    ).astype(jnp.float32)
    context_grad = jnp.einsum(
        "rd,cd->rc",
        mixed_grad,
        lax.all_gather(out_weight, "fsdp", axis=0, tiled=True),
        preferred_element_type=jnp.float32,
    ).astype(jnp.bfloat16)
    frame_grad = attend_back(frames, soft_probs, rounded, context_grad)
    slot_total = incoming.shape[0]
    back_index = jnp.where(filled, compute_src, slot_total)
    returning = jnp.zeros_like(incoming).at[back_index].set(frame_grad, mode="drop")
    arrived = lax.all_to_all(returning, "dp", split_axis=0, concat_axis=0, tiled=True)
    source_index = jnp.where(present, send_rows, row_count)
    projected_grad = jnp.zeros_like(projected).at[source_index].set(arrived, mode="drop")
    scale_factor = (row_count * lax.axis_size("dp") * lax.axis_size("fsdp")) ** (-0.5)
    kernel_piece = fsdp_sum_rows(kernel_part)
    owned_rows = weight_share.shape[0]
    both = dp_allreduce_a2a(jnp.concatenate([weight_share, kernel_piece], axis=0))
    weight_total = both[:owned_rows]
    kernel_total = lax.all_gather(both[owned_rows:], "fsdp", axis=0, tiled=True)[: kernel.shape[0]]
    return (
        result.astype(jnp.bfloat16),
        projected_grad,
        weight_total * scale_factor,
        kernel_total * scale_factor,
    )


def fsdp_sum_rows(x):
    n = lax.axis_size("fsdp")
    per = -(-x.shape[0] // n)
    padded = jnp.pad(x, ((0, n * per - x.shape[0]), (0, 0)))
    got = lax.all_to_all(padded.reshape(n, per, x.shape[1]), "fsdp", split_axis=0, concat_axis=0, tiled=True)
    return jnp.sum(got, axis=0)


def dp_allreduce_a2a(x):
    n = lax.axis_size("dp")
    per = -(-x.shape[0] // n)
    padded = jnp.pad(x, ((0, n * per - x.shape[0]), (0, 0))).reshape(n, per, x.shape[1])
    got = lax.all_to_all(padded, "dp", split_axis=0, concat_axis=0, tiled=True)
    part = jnp.sum(got, axis=0, keepdims=True)
    whole = exchange_gather(part[0], "dp")
    return whole.reshape(n * per, x.shape[1])[: x.shape[0]]


def exchange_gather(piece, axis):
    count = lax.axis_size(axis)
    assert count & (count - 1) == 0
    index = lax.axis_index(axis)
    blocks = piece[None]
    distance = 1
    while distance < count:
        pairs = [(source, source ^ distance) for source in range(count)]
        other = lax.ppermute(blocks, axis, pairs)
        upper = (index // distance) % 2 == 1
        blocks = jnp.where(
            upper, jnp.concatenate([other, blocks], axis=0), jnp.concatenate([blocks, other], axis=0)
        )
        distance *= 2
    return blocks

def solution(mesh):
    placed = (
        P(("dp", "fsdp"), None),
        P("fsdp", None),
        P(),
        P(("dp", "fsdp"), None),
        P(("dp", "fsdp")),
        P(("dp", "fsdp")),
        P(("dp", "fsdp")),
    )
    return jax.shard_map(
        body,
        mesh=mesh,
        in_specs=placed,
        out_specs=(P(("dp", "fsdp"), None), P(("dp", "fsdp"), None), P("fsdp", None), P()),
        check_vma=False,
    )
```

```python
import jax
import jax.numpy as jnp
from jax import lax
from jax.sharding import Mesh, PartitionSpec as P

DP = ("dz", "dx")
FSDP = ("fy", "fc")

HEADS = 8
HEAD_DIM = 96


def split_heads(frames):
    length = frames.shape[0]
    inner_width = HEADS * HEAD_DIM
    query_part = frames[:, :inner_width].reshape(length, HEADS, HEAD_DIM)
    key_part = frames[:, inner_width : 2 * inner_width].reshape(length, HEADS, HEAD_DIM)
    value_part = frames[:, 2 * inner_width :].reshape(length, HEADS, HEAD_DIM)
    return (query_part, key_part, value_part)


def attend(frames, segment):
    query_part, key_part, value_part = split_heads(frames)
    scores = jnp.einsum(
        "qhd,khd->hqk", query_part, key_part, preferred_element_type=jnp.float32
    ) * HEAD_DIM ** (-0.5)
    inside = segment[:, None] == segment[None, :]
    scores = jnp.where(inside[None], scores, -1e30)
    highest = jnp.max(scores, axis=2, keepdims=True)
    weights = jnp.exp(scores - highest)
    soft_probs = weights / jnp.sum(weights, axis=2, keepdims=True)
    rounded = soft_probs.astype(jnp.bfloat16)
    context = jnp.einsum("hqk,khd->qhd", rounded, value_part, preferred_element_type=jnp.float32)
    return (
        context.reshape(frames.shape[0], HEADS * HEAD_DIM).astype(jnp.bfloat16),
        soft_probs,
        rounded,
    )


def attend_back(frames, soft_probs, rounded, context_grad):
    query_part, key_part, value_part = split_heads(frames)
    length = frames.shape[0]
    inner_width = HEADS * HEAD_DIM
    upstream = context_grad.reshape(length, HEADS, HEAD_DIM)
    value_grad = jnp.einsum("hqk,qhd->khd", rounded, upstream, preferred_element_type=jnp.float32)
    prob_grad = jnp.einsum("qhd,khd->hqk", upstream, value_part, preferred_element_type=jnp.float32)
    score_grad = soft_probs * (prob_grad - jnp.sum(prob_grad * soft_probs, axis=2, keepdims=True))
    score_grad = (score_grad * HEAD_DIM ** (-0.5)).astype(jnp.bfloat16)
    query_grad = jnp.einsum(
        "hqk,khd->qhd", score_grad, key_part, preferred_element_type=jnp.float32
    )
    key_grad = jnp.einsum(
        "hqk,qhd->khd", score_grad, query_part, preferred_element_type=jnp.float32
    )
    return jnp.concatenate(
        [
            query_grad.reshape(length, inner_width).astype(jnp.bfloat16),
            key_grad.reshape(length, inner_width).astype(jnp.bfloat16),
            value_grad.reshape(length, inner_width).astype(jnp.bfloat16),
        ],
        axis=1,
    )


def finish(mixed, kernel, segment):
    length = mixed.shape[0]
    tap_count = kernel.shape[0]
    half_span = (tap_count - 1) // 2
    signal = mixed.astype(jnp.float32)
    padded = jnp.pad(signal, ((half_span, half_span), (0, 0)))
    neighbours = jnp.pad(segment, (half_span, half_span), constant_values=-2)
    convolved = jnp.zeros_like(signal)
    for offset in range(tap_count):
        matching = (neighbours[offset : offset + length] == segment).astype(jnp.float32)
        convolved = (
            convolved + kernel[offset] * padded[offset : offset + length] * matching[:, None]
        )
    return signal + jax.nn.silu(convolved)


def body(projected, out_weight, kernel, cotangent, send_rows, compute_src, segment):
    row_count = projected.shape[0]
    present = send_rows >= 0
    outgoing = jnp.take(projected, jnp.maximum(send_rows, 0), axis=0)
    outgoing = jnp.where(present[:, None], outgoing, jnp.zeros_like(outgoing))
    incoming = lax.all_to_all(outgoing, DP, split_axis=0, concat_axis=0, tiled=True)
    filled = compute_src >= 0
    frames = jnp.take(incoming, jnp.maximum(compute_src, 0), axis=0)
    frames = jnp.where(filled[:, None], frames, jnp.zeros_like(frames))
    context, soft_probs, rounded = attend(frames, segment)
    columns = context
    mixed_sums = jnp.dot(
        columns,
        lax.all_gather(out_weight, FSDP, axis=0, tiled=True),
        preferred_element_type=jnp.float32,
    )
    mixed = mixed_sums.astype(jnp.bfloat16)
    result, pullback = jax.vjp(
        lambda signal, kernel_taps: finish(signal, kernel_taps, segment), mixed, kernel
    )
    mixed_grad, kernel_part = pullback(cotangent.astype(jnp.float32))
    columns = context
    weight_share = lax.psum_scatter(
        jnp.einsum("rc,rd->cd", columns, mixed_grad, preferred_element_type=jnp.float32).astype(
            jnp.bfloat16
        ),
        FSDP,
        scatter_dimension=0,
        tiled=True,
    ).astype(jnp.float32)
    context_grad = jnp.einsum(
        "rd,cd->rc",
        mixed_grad,
        lax.all_gather(out_weight, FSDP, axis=0, tiled=True),
        preferred_element_type=jnp.float32,
    ).astype(jnp.bfloat16)
    frame_grad = attend_back(frames, soft_probs, rounded, context_grad)
    slot_total = incoming.shape[0]
    back_index = jnp.where(filled, compute_src, slot_total)
    returning = jnp.zeros_like(incoming).at[back_index].set(frame_grad, mode="drop")
    arrived = lax.all_to_all(returning, DP, split_axis=0, concat_axis=0, tiled=True)
    source_index = jnp.where(present, send_rows, row_count)
    projected_grad = jnp.zeros_like(projected).at[source_index].set(arrived, mode="drop")
    scale_factor = (row_count * lax.axis_size(DP) * lax.axis_size(FSDP)) ** (-0.5)
    kernel_piece = sum_rows(kernel_part, FSDP)
    owned_rows = weight_share.shape[0]
    both = jnp.concatenate([weight_share, kernel_piece], axis=0)
    inner = sum_rows(both, "dx")
    inner_rows = inner.shape[0]
    inner = gather_rows(sum_rows(inner, "dz"), "dz")[:inner_rows]
    both = gather_rows(inner, "dx")[: both.shape[0]]
    weight_total = both[:owned_rows]
    kernel_total = gather_rows(gather_rows(both[owned_rows:], "fc"), "fy")[: kernel.shape[0]]

    return (
        result.astype(jnp.bfloat16),
        projected_grad,
        weight_total * scale_factor,
        kernel_total * scale_factor,
    )


def sum_rows(x, axis):
    count = lax.axis_size(axis)
    per = -(-x.shape[0] // count)
    padded = jnp.pad(x, ((0, count * per - x.shape[0]), (0, 0)))
    got = lax.all_to_all(padded.reshape(count, per, x.shape[1]), axis, split_axis=0, concat_axis=0, tiled=True)
    return jnp.sum(got, axis=0)


def gather_rows(piece, axis):
    return lax.all_gather(piece, axis, axis=0, tiled=True)

def solution(mesh):
    dp_count, fsdp_count = mesh.devices.shape
    fine = Mesh(
        mesh.devices.reshape(dp_count // 4, 4, fsdp_count // 2, 2), ("dz", "dx", "fy", "fc")
    )
    placed = (
        P((*DP, *FSDP), None),
        P(FSDP, None),
        P(),
        P((*DP, *FSDP), None),
        P((*DP, *FSDP)),
        P((*DP, *FSDP)),
        P((*DP, *FSDP)),
    )
    return jax.shard_map(
        body,
        mesh=fine,
        in_specs=placed,
        out_specs=(P((*DP, *FSDP), None), P((*DP, *FSDP), None), P(FSDP, None), P()),
        check_vma=False,
    )
```

```python
import jax
import jax.numpy as jnp
from jax import lax
from jax.sharding import Mesh, PartitionSpec as P

DP = ("dz", "dx")
FSDP = ("fy", "fc")

HEADS = 8
HEAD_DIM = 96


def split_heads(frames):
    length = frames.shape[0]
    inner_width = HEADS * HEAD_DIM
    query_part = frames[:, :inner_width].reshape(length, HEADS, HEAD_DIM)
    key_part = frames[:, inner_width : 2 * inner_width].reshape(length, HEADS, HEAD_DIM)
    value_part = frames[:, 2 * inner_width :].reshape(length, HEADS, HEAD_DIM)
    return (query_part, key_part, value_part)


def attend(frames, segment):
    query_part, key_part, value_part = split_heads(frames)
    scores = jnp.einsum(
        "qhd,khd->hqk", query_part, key_part, preferred_element_type=jnp.float32
    ) * HEAD_DIM ** (-0.5)
    inside = segment[:, None] == segment[None, :]
    scores = jnp.where(inside[None], scores, -1e30)
    highest = jnp.max(scores, axis=2, keepdims=True)
    weights = jnp.exp(scores - highest)
    soft_probs = weights / jnp.sum(weights, axis=2, keepdims=True)
    rounded = soft_probs.astype(jnp.bfloat16)
    context = jnp.einsum("hqk,khd->qhd", rounded, value_part, preferred_element_type=jnp.float32)
    return (
        context.reshape(frames.shape[0], HEADS * HEAD_DIM).astype(jnp.bfloat16),
        soft_probs,
        rounded,
    )


def attend_back(frames, soft_probs, rounded, context_grad):
    query_part, key_part, value_part = split_heads(frames)
    length = frames.shape[0]
    inner_width = HEADS * HEAD_DIM
    upstream = context_grad.reshape(length, HEADS, HEAD_DIM)
    value_grad = jnp.einsum("hqk,qhd->khd", rounded, upstream, preferred_element_type=jnp.float32)
    prob_grad = jnp.einsum("qhd,khd->hqk", upstream, value_part, preferred_element_type=jnp.float32)
    score_grad = soft_probs * (prob_grad - jnp.sum(prob_grad * soft_probs, axis=2, keepdims=True))
    score_grad = (score_grad * HEAD_DIM ** (-0.5)).astype(jnp.bfloat16)
    query_grad = jnp.einsum(
        "hqk,khd->qhd", score_grad, key_part, preferred_element_type=jnp.float32
    )
    key_grad = jnp.einsum(
        "hqk,qhd->khd", score_grad, query_part, preferred_element_type=jnp.float32
    )
    return jnp.concatenate(
        [
            query_grad.reshape(length, inner_width).astype(jnp.bfloat16),
            key_grad.reshape(length, inner_width).astype(jnp.bfloat16),
            value_grad.reshape(length, inner_width).astype(jnp.bfloat16),
        ],
        axis=1,
    )


def finish(mixed, kernel, segment):
    length = mixed.shape[0]
    tap_count = kernel.shape[0]
    half_span = (tap_count - 1) // 2
    signal = mixed.astype(jnp.float32)
    padded = jnp.pad(signal, ((half_span, half_span), (0, 0)))
    neighbours = jnp.pad(segment, (half_span, half_span), constant_values=-2)
    convolved = jnp.zeros_like(signal)
    for offset in range(tap_count):
        matching = (neighbours[offset : offset + length] == segment).astype(jnp.float32)
        convolved = (
            convolved + kernel[offset] * padded[offset : offset + length] * matching[:, None]
        )
    return signal + jax.nn.silu(convolved)


def body(projected, out_weight, kernel, cotangent, send_rows, compute_src, segment):
    row_count = projected.shape[0]
    present = send_rows >= 0
    outgoing = jnp.take(projected, jnp.maximum(send_rows, 0), axis=0)
    outgoing = jnp.where(present[:, None], outgoing, jnp.zeros_like(outgoing))
    incoming = lax.all_to_all(outgoing, DP, split_axis=0, concat_axis=0, tiled=True)
    filled = compute_src >= 0
    frames = jnp.take(incoming, jnp.maximum(compute_src, 0), axis=0)
    frames = jnp.where(filled[:, None], frames, jnp.zeros_like(frames))
    context, soft_probs, rounded = attend(frames, segment)
    columns = context
    mixed_sums = jnp.dot(
        columns,
        lax.all_gather(out_weight, FSDP, axis=0, tiled=True),
        preferred_element_type=jnp.float32,
    )
    mixed = mixed_sums.astype(jnp.bfloat16)
    result, pullback = jax.vjp(
        lambda signal, kernel_taps: finish(signal, kernel_taps, segment), mixed, kernel
    )
    mixed_grad, kernel_part = pullback(cotangent.astype(jnp.float32))
    columns = context
    weight_share = lax.psum_scatter(
        jnp.einsum("rc,rd->cd", columns, mixed_grad, preferred_element_type=jnp.float32).astype(
            jnp.bfloat16
        ),
        FSDP,
        scatter_dimension=0,
        tiled=True,
    ).astype(jnp.float32)
    context_grad = jnp.einsum(
        "rd,cd->rc",
        mixed_grad,
        lax.all_gather(out_weight, FSDP, axis=0, tiled=True),
        preferred_element_type=jnp.float32,
    ).astype(jnp.bfloat16)
    frame_grad = attend_back(frames, soft_probs, rounded, context_grad)
    slot_total = incoming.shape[0]
    back_index = jnp.where(filled, compute_src, slot_total)
    returning = jnp.zeros_like(incoming).at[back_index].set(frame_grad, mode="drop")
    arrived = lax.all_to_all(returning, DP, split_axis=0, concat_axis=0, tiled=True)
    source_index = jnp.where(present, send_rows, row_count)
    projected_grad = jnp.zeros_like(projected).at[source_index].set(arrived, mode="drop")
    scale_factor = (row_count * lax.axis_size(DP) * lax.axis_size(FSDP)) ** (-0.5)
    weight_share, arrived = lax.optimization_barrier((weight_share, arrived))
    kernel_piece = sum_rows(kernel_part, FSDP)
    owned_rows = weight_share.shape[0]
    both = jnp.concatenate([weight_share, kernel_piece], axis=0)
    inner = sum_rows(both, "dx")
    inner_rows = inner.shape[0]
    inner = gather_rows(sum_rows(inner, "dz"), "dz")[:inner_rows]
    both = gather_rows(inner, "dx")[: both.shape[0]]
    weight_total = both[:owned_rows]
    kernel_total = gather_rows(gather_rows(both[owned_rows:], "fc"), "fy")[: kernel.shape[0]]

    return (
        result.astype(jnp.bfloat16),
        projected_grad,
        weight_total * scale_factor,
        kernel_total * scale_factor,
    )


def sum_rows(x, axis):
    count = lax.axis_size(axis)
    per = -(-x.shape[0] // count)
    padded = jnp.pad(x, ((0, count * per - x.shape[0]), (0, 0)))
    got = lax.all_to_all(padded.reshape(count, per, x.shape[1]), axis, split_axis=0, concat_axis=0, tiled=True)
    return jnp.sum(got, axis=0)


def gather_rows(piece, axis):
    count = lax.axis_size(axis)
    copies = jnp.broadcast_to(piece[None], (count, *piece.shape))
    got = lax.all_to_all(copies, axis, split_axis=0, concat_axis=0, tiled=True)
    return got.reshape(count * piece.shape[0], piece.shape[1])

def solution(mesh):
    dp_count, fsdp_count = mesh.devices.shape
    fine = Mesh(
        mesh.devices.reshape(dp_count // 4, 4, fsdp_count // 2, 2), ("dz", "dx", "fy", "fc")
    )
    placed = (
        P((*DP, *FSDP), None),
        P(FSDP, None),
        P(),
        P((*DP, *FSDP), None),
        P((*DP, *FSDP)),
        P((*DP, *FSDP)),
        P((*DP, *FSDP)),
    )
    return jax.shard_map(
        body,
        mesh=fine,
        in_specs=placed,
        out_specs=(P((*DP, *FSDP), None), P((*DP, *FSDP), None), P(FSDP, None), P()),
        check_vma=False,
    )
```

```python
import jax
import jax.numpy as jnp
from jax import lax
from jax.sharding import Mesh, PartitionSpec as P

DP = ("dz", "dx")
FSDP = ("fy", "fc")

HEADS = 8
HEAD_DIM = 96


def split_heads(frames):
    length = frames.shape[0]
    inner_width = HEADS * HEAD_DIM
    query_part = frames[:, :inner_width].reshape(length, HEADS, HEAD_DIM)
    key_part = frames[:, inner_width : 2 * inner_width].reshape(length, HEADS, HEAD_DIM)
    value_part = frames[:, 2 * inner_width :].reshape(length, HEADS, HEAD_DIM)
    return (query_part, key_part, value_part)


def attend(frames, segment):
    query_part, key_part, value_part = split_heads(frames)
    scores = jnp.einsum(
        "qhd,khd->hqk", query_part, key_part, preferred_element_type=jnp.float32
    ) * HEAD_DIM ** (-0.5)
    inside = segment[:, None] == segment[None, :]
    scores = jnp.where(inside[None], scores, -1e30)
    highest = jnp.max(scores, axis=2, keepdims=True)
    weights = jnp.exp(scores - highest)
    soft_probs = weights / jnp.sum(weights, axis=2, keepdims=True)
    rounded = soft_probs.astype(jnp.bfloat16)
    context = jnp.einsum("hqk,khd->qhd", rounded, value_part, preferred_element_type=jnp.float32)
    return (
        context.reshape(frames.shape[0], HEADS * HEAD_DIM).astype(jnp.bfloat16),
        soft_probs,
        rounded,
    )


def attend_back(frames, soft_probs, rounded, context_grad):
    query_part, key_part, value_part = split_heads(frames)
    length = frames.shape[0]
    inner_width = HEADS * HEAD_DIM
    upstream = context_grad.reshape(length, HEADS, HEAD_DIM)
    value_grad = jnp.einsum("hqk,qhd->khd", rounded, upstream, preferred_element_type=jnp.float32)
    prob_grad = jnp.einsum("qhd,khd->hqk", upstream, value_part, preferred_element_type=jnp.float32)
    score_grad = soft_probs * (prob_grad - jnp.sum(prob_grad * soft_probs, axis=2, keepdims=True))
    score_grad = (score_grad * HEAD_DIM ** (-0.5)).astype(jnp.bfloat16)
    query_grad = jnp.einsum(
        "hqk,khd->qhd", score_grad, key_part, preferred_element_type=jnp.float32
    )
    key_grad = jnp.einsum(
        "hqk,qhd->khd", score_grad, query_part, preferred_element_type=jnp.float32
    )
    return jnp.concatenate(
        [
            query_grad.reshape(length, inner_width).astype(jnp.bfloat16),
            key_grad.reshape(length, inner_width).astype(jnp.bfloat16),
            value_grad.reshape(length, inner_width).astype(jnp.bfloat16),
        ],
        axis=1,
    )


def finish(mixed, kernel, segment):
    length = mixed.shape[0]
    tap_count = kernel.shape[0]
    half_span = (tap_count - 1) // 2
    signal = mixed.astype(jnp.float32)
    padded = jnp.pad(signal, ((half_span, half_span), (0, 0)))
    neighbours = jnp.pad(segment, (half_span, half_span), constant_values=-2)
    convolved = jnp.zeros_like(signal)
    for offset in range(tap_count):
        matching = (neighbours[offset : offset + length] == segment).astype(jnp.float32)
        convolved = (
            convolved + kernel[offset] * padded[offset : offset + length] * matching[:, None]
        )
    return signal + jax.nn.silu(convolved)


def body(projected, out_weight, kernel, cotangent, send_rows, compute_src, segment):
    row_count = projected.shape[0]
    present = send_rows >= 0
    outgoing = jnp.take(projected, jnp.maximum(send_rows, 0), axis=0)
    outgoing = jnp.where(present[:, None], outgoing, jnp.zeros_like(outgoing))
    incoming = lax.all_to_all(outgoing, DP, split_axis=0, concat_axis=0, tiled=True)
    filled = compute_src >= 0
    frames = jnp.take(incoming, jnp.maximum(compute_src, 0), axis=0)
    frames = jnp.where(filled[:, None], frames, jnp.zeros_like(frames))
    context, soft_probs, rounded = attend(frames, segment)
    columns = context
    mixed_sums = jnp.dot(
        columns,
        lax.all_gather(out_weight, FSDP, axis=0, tiled=True),
        preferred_element_type=jnp.float32,
    )
    mixed = mixed_sums.astype(jnp.bfloat16)
    result, pullback = jax.vjp(
        lambda signal, kernel_taps: finish(signal, kernel_taps, segment), mixed, kernel
    )
    mixed_grad, kernel_part = pullback(cotangent.astype(jnp.float32))
    columns = context
    weight_share = lax.psum_scatter(
        jnp.einsum("rc,rd->cd", columns, mixed_grad, preferred_element_type=jnp.float32).astype(
            jnp.bfloat16
        ),
        FSDP,
        scatter_dimension=0,
        tiled=True,
    ).astype(jnp.float32)
    context_grad = jnp.einsum(
        "rd,cd->rc",
        mixed_grad,
        lax.all_gather(out_weight, FSDP, axis=0, tiled=True),
        preferred_element_type=jnp.float32,
    ).astype(jnp.bfloat16)
    frame_grad = attend_back(frames, soft_probs, rounded, context_grad)
    slot_total = incoming.shape[0]
    back_index = jnp.where(filled, compute_src, slot_total)
    returning = jnp.zeros_like(incoming).at[back_index].set(frame_grad, mode="drop")
    arrived = lax.all_to_all(returning, DP, split_axis=0, concat_axis=0, tiled=True)
    source_index = jnp.where(present, send_rows, row_count)
    projected_grad = jnp.zeros_like(projected).at[source_index].set(arrived, mode="drop")
    scale_factor = (row_count * lax.axis_size(DP) * lax.axis_size(FSDP)) ** (-0.5)
    kernel_total = reduce_rows(sum_rows(kernel_part, FSDP))
    kernel_total = gather_rows(gather_rows(kernel_total, "fc"), "fy")[: kernel.shape[0]]
    weight_share, arrived, kernel_total = lax.optimization_barrier((weight_share, arrived, kernel_total))
    weight_total = reduce_rows(weight_share)

    return (
        result.astype(jnp.bfloat16),
        projected_grad,
        weight_total * scale_factor,
        kernel_total * scale_factor,
    )


def sum_rows(x, axis):
    count = lax.axis_size(axis)
    per = -(-x.shape[0] // count)
    padded = jnp.pad(x, ((0, count * per - x.shape[0]), (0, 0)))
    got = lax.all_to_all(padded.reshape(count, per, x.shape[1]), axis, split_axis=0, concat_axis=0, tiled=True)
    return jnp.sum(got, axis=0)


def gather_rows(piece, axis):
    count = lax.axis_size(axis)
    copies = jnp.broadcast_to(piece[None], (count, *piece.shape))
    got = lax.all_to_all(copies, axis, split_axis=0, concat_axis=0, tiled=True)
    return got.reshape(count * piece.shape[0], piece.shape[1])


def reduce_rows(x):
    inner = sum_rows(x, "dx")
    inner_rows = inner.shape[0]
    inner = gather_rows(sum_rows(inner, "dz"), "dz")[:inner_rows]
    return gather_rows(inner, "dx")[: x.shape[0]]

def solution(mesh):
    dp_count, fsdp_count = mesh.devices.shape
    fine = Mesh(
        mesh.devices.reshape(dp_count // 4, 4, fsdp_count // 2, 2), ("dz", "dx", "fy", "fc")
    )
    placed = (
        P((*DP, *FSDP), None),
        P(FSDP, None),
        P(),
        P((*DP, *FSDP), None),
        P((*DP, *FSDP)),
        P((*DP, *FSDP)),
        P((*DP, *FSDP)),
    )
    return jax.shard_map(
        body,
        mesh=fine,
        in_specs=placed,
        out_specs=(P((*DP, *FSDP), None), P((*DP, *FSDP), None), P(FSDP, None), P()),
        check_vma=False,
    )
```

```python
import jax
import jax.numpy as jnp
from jax import lax
from jax.sharding import Mesh, PartitionSpec as P

DP = ("dz", "dx")
FSDP = ("fy", "fc")

HEADS = 8
HEAD_DIM = 96


def split_heads(frames):
    length = frames.shape[0]
    inner_width = HEADS * HEAD_DIM
    query_part = frames[:, :inner_width].reshape(length, HEADS, HEAD_DIM)
    key_part = frames[:, inner_width : 2 * inner_width].reshape(length, HEADS, HEAD_DIM)
    value_part = frames[:, 2 * inner_width :].reshape(length, HEADS, HEAD_DIM)
    return (query_part, key_part, value_part)


def attend(frames, segment):
    query_part, key_part, value_part = split_heads(frames)
    scores = jnp.einsum(
        "qhd,khd->hqk", query_part, key_part, preferred_element_type=jnp.float32
    ) * HEAD_DIM ** (-0.5)
    inside = segment[:, None] == segment[None, :]
    scores = jnp.where(inside[None], scores, -1e30)
    highest = jnp.max(scores, axis=2, keepdims=True)
    weights = jnp.exp(scores - highest)
    soft_probs = weights / jnp.sum(weights, axis=2, keepdims=True)
    rounded = soft_probs.astype(jnp.bfloat16)
    context = jnp.einsum("hqk,khd->qhd", rounded, value_part, preferred_element_type=jnp.float32)
    return (
        context.reshape(frames.shape[0], HEADS * HEAD_DIM).astype(jnp.bfloat16),
        soft_probs,
        rounded,
    )


def attend_back(frames, soft_probs, rounded, context_grad):
    query_part, key_part, value_part = split_heads(frames)
    length = frames.shape[0]
    inner_width = HEADS * HEAD_DIM
    upstream = context_grad.reshape(length, HEADS, HEAD_DIM)
    value_grad = jnp.einsum("hqk,qhd->khd", rounded, upstream, preferred_element_type=jnp.float32)
    prob_grad = jnp.einsum("qhd,khd->hqk", upstream, value_part, preferred_element_type=jnp.float32)
    score_grad = soft_probs * (prob_grad - jnp.sum(prob_grad * soft_probs, axis=2, keepdims=True))
    score_grad = (score_grad * HEAD_DIM ** (-0.5)).astype(jnp.bfloat16)
    query_grad = jnp.einsum(
        "hqk,khd->qhd", score_grad, key_part, preferred_element_type=jnp.float32
    )
    key_grad = jnp.einsum(
        "hqk,qhd->khd", score_grad, query_part, preferred_element_type=jnp.float32
    )
    return jnp.concatenate(
        [
            query_grad.reshape(length, inner_width).astype(jnp.bfloat16),
            key_grad.reshape(length, inner_width).astype(jnp.bfloat16),
            value_grad.reshape(length, inner_width).astype(jnp.bfloat16),
        ],
        axis=1,
    )


def finish(mixed, kernel, segment):
    length = mixed.shape[0]
    tap_count = kernel.shape[0]
    half_span = (tap_count - 1) // 2
    signal = mixed.astype(jnp.float32)
    padded = jnp.pad(signal, ((half_span, half_span), (0, 0)))
    neighbours = jnp.pad(segment, (half_span, half_span), constant_values=-2)
    convolved = jnp.zeros_like(signal)
    for offset in range(tap_count):
        matching = (neighbours[offset : offset + length] == segment).astype(jnp.float32)
        convolved = (
            convolved + kernel[offset] * padded[offset : offset + length] * matching[:, None]
        )
    return signal + jax.nn.silu(convolved)


def body(projected, out_weight, kernel, cotangent, send_rows, compute_src, segment):
    row_count = projected.shape[0]
    present = send_rows >= 0
    outgoing = jnp.take(projected, jnp.maximum(send_rows, 0), axis=0)
    outgoing = jnp.where(present[:, None], outgoing, jnp.zeros_like(outgoing))
    incoming = lax.all_to_all(outgoing, DP, split_axis=0, concat_axis=0, tiled=True)
    filled = compute_src >= 0
    frames = jnp.take(incoming, jnp.maximum(compute_src, 0), axis=0)
    frames = jnp.where(filled[:, None], frames, jnp.zeros_like(frames))
    context, soft_probs, rounded = attend(frames, segment)
    columns = context
    mixed_sums = jnp.dot(
        columns,
        lax.all_gather(out_weight, FSDP, axis=0, tiled=True),
        preferred_element_type=jnp.float32,
    )
    mixed = mixed_sums.astype(jnp.bfloat16)
    result, pullback = jax.vjp(
        lambda signal, kernel_taps: finish(signal, kernel_taps, segment), mixed, kernel
    )
    mixed_grad, kernel_part = pullback(cotangent.astype(jnp.float32))
    columns = context
    weight_share = lax.psum_scatter(
        jnp.einsum("rc,rd->cd", columns, mixed_grad, preferred_element_type=jnp.float32).astype(
            jnp.bfloat16
        ),
        FSDP,
        scatter_dimension=0,
        tiled=True,
    ).astype(jnp.float32)
    context_grad = jnp.einsum(
        "rd,cd->rc",
        mixed_grad,
        lax.all_gather(out_weight, FSDP, axis=0, tiled=True),
        preferred_element_type=jnp.float32,
    ).astype(jnp.bfloat16)
    frame_grad = attend_back(frames, soft_probs, rounded, context_grad)
    slot_total = incoming.shape[0]
    back_index = jnp.where(filled, compute_src, slot_total)
    returning = jnp.zeros_like(incoming).at[back_index].set(frame_grad, mode="drop")
    arrived = lax.all_to_all(returning, DP, split_axis=0, concat_axis=0, tiled=True)
    source_index = jnp.where(present, send_rows, row_count)
    projected_grad = jnp.zeros_like(projected).at[source_index].set(arrived, mode="drop")
    scale_factor = (row_count * lax.axis_size(DP) * lax.axis_size(FSDP)) ** (-0.5)
    weight_share, arrived = lax.optimization_barrier((weight_share, arrived))
    kernel_piece = sum_rows(kernel_part, FSDP)
    owned_rows = weight_share.shape[0]
    both = jnp.concatenate([weight_share, kernel_piece], axis=0)
    piece = sum_rows(both, DP)
    both = gather_rows(gather_rows(piece, "dx"), "dz")[: both.shape[0]]
    weight_total = both[:owned_rows]
    kernel_total = gather_rows(both[owned_rows:], FSDP)[: kernel.shape[0]]

    return (
        result.astype(jnp.bfloat16),
        projected_grad,
        weight_total * scale_factor,
        kernel_total * scale_factor,
    )


def sum_rows(x, axis):
    count = lax.axis_size(axis)
    per = -(-x.shape[0] // count)
    padded = jnp.pad(x, ((0, count * per - x.shape[0]), (0, 0)))
    got = lax.all_to_all(padded.reshape(count, per, x.shape[1]), axis, split_axis=0, concat_axis=0, tiled=True)
    return jnp.sum(got, axis=0)


def gather_rows(piece, axis):
    count = lax.axis_size(axis)
    copies = jnp.broadcast_to(piece[None], (count, *piece.shape))
    got = lax.all_to_all(copies, axis, split_axis=0, concat_axis=0, tiled=True)
    return got.reshape(count * piece.shape[0], piece.shape[1])

def solution(mesh):
    dp_count, fsdp_count = mesh.devices.shape
    fine = Mesh(
        mesh.devices.reshape(dp_count // 4, 4, fsdp_count // 2, 2), ("dz", "dx", "fy", "fc")
    )
    placed = (
        P((*DP, *FSDP), None),
        P(FSDP, None),
        P(),
        P((*DP, *FSDP), None),
        P((*DP, *FSDP)),
        P((*DP, *FSDP)),
        P((*DP, *FSDP)),
    )
    return jax.shard_map(
        body,
        mesh=fine,
        in_specs=placed,
        out_specs=(P((*DP, *FSDP), None), P((*DP, *FSDP), None), P(FSDP, None), P()),
        check_vma=False,
    )
```

```python
import jax
import jax.numpy as jnp
from jax import lax
from jax.sharding import Mesh, PartitionSpec as P

DP = ("dz", "dx")
FSDP = ("fy", "fc")

HEADS = 8
HEAD_DIM = 96


def split_heads(frames):
    length = frames.shape[0]
    inner_width = HEADS * HEAD_DIM
    query_part = frames[:, :inner_width].reshape(length, HEADS, HEAD_DIM)
    key_part = frames[:, inner_width : 2 * inner_width].reshape(length, HEADS, HEAD_DIM)
    value_part = frames[:, 2 * inner_width :].reshape(length, HEADS, HEAD_DIM)
    return (query_part, key_part, value_part)


def attend(frames, segment):
    query_part, key_part, value_part = split_heads(frames)
    scores = jnp.einsum(
        "qhd,khd->hqk", query_part, key_part, preferred_element_type=jnp.float32
    ) * HEAD_DIM ** (-0.5)
    inside = segment[:, None] == segment[None, :]
    scores = jnp.where(inside[None], scores, -1e30)
    highest = jnp.max(scores, axis=2, keepdims=True)
    weights = jnp.exp(scores - highest)
    soft_probs = weights / jnp.sum(weights, axis=2, keepdims=True)
    rounded = soft_probs.astype(jnp.bfloat16)
    context = jnp.einsum("hqk,khd->qhd", rounded, value_part, preferred_element_type=jnp.float32)
    return (
        context.reshape(frames.shape[0], HEADS * HEAD_DIM).astype(jnp.bfloat16),
        soft_probs,
        rounded,
    )


def attend_back(frames, soft_probs, rounded, context_grad):
    query_part, key_part, value_part = split_heads(frames)
    length = frames.shape[0]
    inner_width = HEADS * HEAD_DIM
    upstream = context_grad.reshape(length, HEADS, HEAD_DIM)
    value_grad = jnp.einsum("hqk,qhd->khd", rounded, upstream, preferred_element_type=jnp.float32)
    prob_grad = jnp.einsum("qhd,khd->hqk", upstream, value_part, preferred_element_type=jnp.float32)
    score_grad = soft_probs * (prob_grad - jnp.sum(prob_grad * soft_probs, axis=2, keepdims=True))
    score_grad = (score_grad * HEAD_DIM ** (-0.5)).astype(jnp.bfloat16)
    query_grad = jnp.einsum(
        "hqk,khd->qhd", score_grad, key_part, preferred_element_type=jnp.float32
    )
    key_grad = jnp.einsum(
        "hqk,qhd->khd", score_grad, query_part, preferred_element_type=jnp.float32
    )
    return jnp.concatenate(
        [
            query_grad.reshape(length, inner_width).astype(jnp.bfloat16),
            key_grad.reshape(length, inner_width).astype(jnp.bfloat16),
            value_grad.reshape(length, inner_width).astype(jnp.bfloat16),
        ],
        axis=1,
    )


def finish(mixed, kernel, segment):
    length = mixed.shape[0]
    tap_count = kernel.shape[0]
    half_span = (tap_count - 1) // 2
    signal = mixed.astype(jnp.float32)
    padded = jnp.pad(signal, ((half_span, half_span), (0, 0)))
    neighbours = jnp.pad(segment, (half_span, half_span), constant_values=-2)
    convolved = jnp.zeros_like(signal)
    for offset in range(tap_count):
        matching = (neighbours[offset : offset + length] == segment).astype(jnp.float32)
        convolved = (
            convolved + kernel[offset] * padded[offset : offset + length] * matching[:, None]
        )
    return signal + jax.nn.silu(convolved)


def body(projected, out_weight, kernel, cotangent, send_rows, compute_src, segment):
    row_count = projected.shape[0]
    present = send_rows >= 0
    outgoing = jnp.take(projected, jnp.maximum(send_rows, 0), axis=0)
    outgoing = jnp.where(present[:, None], outgoing, jnp.zeros_like(outgoing))
    incoming = lax.all_to_all(outgoing, DP, split_axis=0, concat_axis=0, tiled=True)
    filled = compute_src >= 0
    frames = jnp.take(incoming, jnp.maximum(compute_src, 0), axis=0)
    frames = jnp.where(filled[:, None], frames, jnp.zeros_like(frames))
    context, soft_probs, rounded = attend(frames, segment)
    columns = context
    mixed_sums = jnp.dot(
        columns,
        lax.all_gather(out_weight, FSDP, axis=0, tiled=True),
        preferred_element_type=jnp.float32,
    )
    mixed = mixed_sums.astype(jnp.bfloat16)
    result, pullback = jax.vjp(
        lambda signal, kernel_taps: finish(signal, kernel_taps, segment), mixed, kernel
    )
    mixed_grad, kernel_part = pullback(cotangent.astype(jnp.float32))
    columns = context
    weight_part = jnp.einsum("rc,rd->cd", columns, mixed_grad, preferred_element_type=jnp.float32)
    weight_share = core_then_chip_sum(weight_part.astype(jnp.bfloat16)).astype(jnp.float32)
    context_grad = jnp.einsum(
        "rd,cd->rc",
        mixed_grad,
        lax.all_gather(out_weight, FSDP, axis=0, tiled=True),
        preferred_element_type=jnp.float32,
    ).astype(jnp.bfloat16)
    frame_grad = attend_back(frames, soft_probs, rounded, context_grad)
    slot_total = incoming.shape[0]
    back_index = jnp.where(filled, compute_src, slot_total)
    returning = jnp.zeros_like(incoming).at[back_index].set(frame_grad, mode="drop")
    arrived = lax.all_to_all(returning, DP, split_axis=0, concat_axis=0, tiled=True)
    source_index = jnp.where(present, send_rows, row_count)
    projected_grad = jnp.zeros_like(projected).at[source_index].set(arrived, mode="drop")
    scale_factor = (row_count * lax.axis_size(DP) * lax.axis_size(FSDP)) ** (-0.5)
    weight_share, arrived = lax.optimization_barrier((weight_share, arrived))
    kernel_piece = sum_rows(kernel_part, FSDP)
    owned_rows = weight_share.shape[0]
    both = jnp.concatenate([weight_share, kernel_piece], axis=0)
    piece = sum_rows(both, DP)
    both = gather_rows(gather_rows(piece, "dx"), "dz")[: both.shape[0]]
    weight_total = both[:owned_rows]
    kernel_total = gather_rows(both[owned_rows:], FSDP)[: kernel.shape[0]]

    return (
        result.astype(jnp.bfloat16),
        projected_grad,
        weight_total * scale_factor,
        kernel_total * scale_factor,
    )


def sum_rows(x, axis):
    count = lax.axis_size(axis)
    per = -(-x.shape[0] // count)
    padded = jnp.pad(x, ((0, count * per - x.shape[0]), (0, 0)))
    got = lax.all_to_all(padded.reshape(count, per, x.shape[1]), axis, split_axis=0, concat_axis=0, tiled=True)
    return jnp.sum(got, axis=0)


def gather_rows(piece, axis):
    count = lax.axis_size(axis)
    copies = jnp.broadcast_to(piece[None], (count, *piece.shape))
    got = lax.all_to_all(copies, axis, split_axis=0, concat_axis=0, tiled=True)
    return got.reshape(count * piece.shape[0], piece.shape[1])


def core_then_chip_sum(x):
    chips, cores = lax.axis_size("fy"), lax.axis_size("fc")
    blocks = x.reshape(chips, cores, x.shape[0] // (chips * cores), x.shape[1]).swapaxes(0, 1)
    got = lax.all_to_all(blocks, "fc", split_axis=0, concat_axis=0, tiled=True)
    summed = jnp.sum(got.astype(jnp.float32), axis=0).astype(x.dtype)
    flat = summed.reshape(-1, x.shape[1])
    return lax.psum_scatter(flat, "fy", scatter_dimension=0, tiled=True)

def solution(mesh):
    dp_count, fsdp_count = mesh.devices.shape
    fine = Mesh(
        mesh.devices.reshape(dp_count // 4, 4, fsdp_count // 2, 2), ("dz", "dx", "fy", "fc")
    )
    placed = (
        P((*DP, *FSDP), None),
        P(FSDP, None),
        P(),
        P((*DP, *FSDP), None),
        P((*DP, *FSDP)),
        P((*DP, *FSDP)),
        P((*DP, *FSDP)),
    )
    return jax.shard_map(
        body,
        mesh=fine,
        in_specs=placed,
        out_specs=(P((*DP, *FSDP), None), P((*DP, *FSDP), None), P(FSDP, None), P()),
        check_vma=False,
    )
```

```python
import jax
import jax.numpy as jnp
from jax import lax
from jax.sharding import Mesh, PartitionSpec as P

DP = ("dz", "dx")
FSDP = ("fy", "fc")

HEADS = 8
HEAD_DIM = 96


def split_heads(frames):
    length = frames.shape[0]
    inner_width = HEADS * HEAD_DIM
    query_part = frames[:, :inner_width].reshape(length, HEADS, HEAD_DIM)
    key_part = frames[:, inner_width : 2 * inner_width].reshape(length, HEADS, HEAD_DIM)
    value_part = frames[:, 2 * inner_width :].reshape(length, HEADS, HEAD_DIM)
    return (query_part, key_part, value_part)


def attend(frames, segment):
    query_part, key_part, value_part = split_heads(frames)
    scores = jnp.einsum(
        "qhd,khd->hqk", query_part, key_part, preferred_element_type=jnp.float32
    ) * HEAD_DIM ** (-0.5)
    inside = segment[:, None] == segment[None, :]
    scores = jnp.where(inside[None], scores, -1e30)
    highest = jnp.max(scores, axis=2, keepdims=True)
    weights = jnp.exp(scores - highest)
    soft_probs = weights / jnp.sum(weights, axis=2, keepdims=True)
    rounded = soft_probs.astype(jnp.bfloat16)
    context = jnp.einsum("hqk,khd->qhd", rounded, value_part, preferred_element_type=jnp.float32)
    return (
        context.reshape(frames.shape[0], HEADS * HEAD_DIM).astype(jnp.bfloat16),
        soft_probs,
        rounded,
    )


def attend_back(frames, soft_probs, rounded, context_grad):
    query_part, key_part, value_part = split_heads(frames)
    length = frames.shape[0]
    inner_width = HEADS * HEAD_DIM
    upstream = context_grad.reshape(length, HEADS, HEAD_DIM)
    value_grad = jnp.einsum("hqk,qhd->khd", rounded, upstream, preferred_element_type=jnp.float32)
    prob_grad = jnp.einsum("qhd,khd->hqk", upstream, value_part, preferred_element_type=jnp.float32)
    score_grad = soft_probs * (prob_grad - jnp.sum(prob_grad * soft_probs, axis=2, keepdims=True))
    score_grad = (score_grad * HEAD_DIM ** (-0.5)).astype(jnp.bfloat16)
    query_grad = jnp.einsum(
        "hqk,khd->qhd", score_grad, key_part, preferred_element_type=jnp.float32
    )
    key_grad = jnp.einsum(
        "hqk,qhd->khd", score_grad, query_part, preferred_element_type=jnp.float32
    )
    return jnp.concatenate(
        [
            query_grad.reshape(length, inner_width).astype(jnp.bfloat16),
            key_grad.reshape(length, inner_width).astype(jnp.bfloat16),
            value_grad.reshape(length, inner_width).astype(jnp.bfloat16),
        ],
        axis=1,
    )


def finish(mixed, kernel, segment):
    length = mixed.shape[0]
    tap_count = kernel.shape[0]
    half_span = (tap_count - 1) // 2
    signal = mixed.astype(jnp.float32)
    padded = jnp.pad(signal, ((half_span, half_span), (0, 0)))
    neighbours = jnp.pad(segment, (half_span, half_span), constant_values=-2)
    convolved = jnp.zeros_like(signal)
    for offset in range(tap_count):
        matching = (neighbours[offset : offset + length] == segment).astype(jnp.float32)
        convolved = (
            convolved + kernel[offset] * padded[offset : offset + length] * matching[:, None]
        )
    return signal + jax.nn.silu(convolved)


def body(projected, out_weight, kernel, cotangent, send_rows, compute_src, segment):
    row_count = projected.shape[0]
    present = send_rows >= 0
    outgoing = jnp.take(projected, jnp.maximum(send_rows, 0), axis=0)
    outgoing = jnp.where(present[:, None], outgoing, jnp.zeros_like(outgoing))
    incoming = lax.all_to_all(outgoing, DP, split_axis=0, concat_axis=0, tiled=True)
    filled = compute_src >= 0
    frames = jnp.take(incoming, jnp.maximum(compute_src, 0), axis=0)
    frames = jnp.where(filled[:, None], frames, jnp.zeros_like(frames))
    context, soft_probs, rounded = attend(frames, segment)
    columns = context
    mixed_sums = jnp.dot(
        columns,
        lax.all_gather(out_weight, FSDP, axis=0, tiled=True),
        preferred_element_type=jnp.float32,
    )
    mixed = mixed_sums.astype(jnp.bfloat16)
    result, pullback = jax.vjp(
        lambda signal, kernel_taps: finish(signal, kernel_taps, segment), mixed, kernel
    )
    mixed_grad, kernel_part = pullback(cotangent.astype(jnp.float32))
    columns = context
    weight_share = lax.psum_scatter(
        jnp.einsum("rc,rd->cd", columns, mixed_grad, preferred_element_type=jnp.float32).astype(
            jnp.bfloat16
        ),
        FSDP,
        scatter_dimension=0,
        tiled=True,
    ).astype(jnp.float32)
    context_grad = jnp.einsum(
        "rd,cd->rc",
        mixed_grad,
        lax.all_gather(out_weight, FSDP, axis=0, tiled=True),
        preferred_element_type=jnp.float32,
    ).astype(jnp.bfloat16)
    frame_grad = attend_back(frames, soft_probs, rounded, context_grad)
    slot_total = incoming.shape[0]
    back_index = jnp.where(filled, compute_src, slot_total)
    returning = jnp.zeros_like(incoming).at[back_index].set(frame_grad, mode="drop")
    arrived = lax.all_to_all(returning, DP, split_axis=0, concat_axis=0, tiled=True)
    source_index = jnp.where(present, send_rows, row_count)
    projected_grad = jnp.zeros_like(projected).at[source_index].set(arrived, mode="drop")
    scale_factor = (row_count * lax.axis_size(DP) * lax.axis_size(FSDP)) ** (-0.5)
    kernel_rows = gather_rows(sum_rows(kernel_part, FSDP), FSDP)[: kernel.shape[0]]
    weight_share, arrived, kernel_rows = lax.optimization_barrier((weight_share, arrived, kernel_rows))
    owned_rows = weight_share.shape[0]
    both = jnp.concatenate([weight_share, kernel_rows], axis=0)
    piece = sum_rows(both, DP)
    both = gather_rows(gather_rows(piece, "dx"), "dz")[: both.shape[0]]
    weight_total = both[:owned_rows]
    kernel_total = both[owned_rows:]

    return (
        result.astype(jnp.bfloat16),
        projected_grad,
        weight_total * scale_factor,
        kernel_total * scale_factor,
    )


def sum_rows(x, axis):
    count = lax.axis_size(axis)
    per = -(-x.shape[0] // count)
    padded = jnp.pad(x, ((0, count * per - x.shape[0]), (0, 0)))
    got = lax.all_to_all(padded.reshape(count, per, x.shape[1]), axis, split_axis=0, concat_axis=0, tiled=True)
    return jnp.sum(got, axis=0)


def gather_rows(piece, axis):
    count = lax.axis_size(axis)
    copies = jnp.broadcast_to(piece[None], (count, *piece.shape))
    got = lax.all_to_all(copies, axis, split_axis=0, concat_axis=0, tiled=True)
    return got.reshape(count * piece.shape[0], piece.shape[1])

def solution(mesh):
    dp_count, fsdp_count = mesh.devices.shape
    fine = Mesh(
        mesh.devices.reshape(dp_count // 4, 4, fsdp_count // 2, 2), ("dz", "dx", "fy", "fc")
    )
    placed = (
        P((*DP, *FSDP), None),
        P(FSDP, None),
        P(),
        P((*DP, *FSDP), None),
        P((*DP, *FSDP)),
        P((*DP, *FSDP)),
        P((*DP, *FSDP)),
    )
    return jax.shard_map(
        body,
        mesh=fine,
        in_specs=placed,
        out_specs=(P((*DP, *FSDP), None), P((*DP, *FSDP), None), P(FSDP, None), P()),
        check_vma=False,
    )
```

```python
import jax
import jax.numpy as jnp
from jax import lax
from jax.sharding import Mesh, PartitionSpec as P

DP = ("dz", "dx")
FSDP = ("fy", "fc")

HEADS = 8
HEAD_DIM = 96


def split_heads(frames):
    length = frames.shape[0]
    inner_width = HEADS * HEAD_DIM
    query_part = frames[:, :inner_width].reshape(length, HEADS, HEAD_DIM)
    key_part = frames[:, inner_width : 2 * inner_width].reshape(length, HEADS, HEAD_DIM)
    value_part = frames[:, 2 * inner_width :].reshape(length, HEADS, HEAD_DIM)
    return (query_part, key_part, value_part)


def attend(frames, segment):
    query_part, key_part, value_part = split_heads(frames)
    scores = jnp.einsum(
        "qhd,khd->hqk", query_part, key_part, preferred_element_type=jnp.float32
    ) * HEAD_DIM ** (-0.5)
    inside = segment[:, None] == segment[None, :]
    scores = jnp.where(inside[None], scores, -1e30)
    highest = jnp.max(scores, axis=2, keepdims=True)
    weights = jnp.exp(scores - highest)
    soft_probs = weights / jnp.sum(weights, axis=2, keepdims=True)
    rounded = soft_probs.astype(jnp.bfloat16)
    context = jnp.einsum("hqk,khd->qhd", rounded, value_part, preferred_element_type=jnp.float32)
    return (
        context.reshape(frames.shape[0], HEADS * HEAD_DIM).astype(jnp.bfloat16),
        soft_probs,
        rounded,
    )


def attend_back(frames, soft_probs, rounded, context_grad):
    query_part, key_part, value_part = split_heads(frames)
    length = frames.shape[0]
    inner_width = HEADS * HEAD_DIM
    upstream = context_grad.reshape(length, HEADS, HEAD_DIM)
    value_grad = jnp.einsum("hqk,qhd->khd", rounded, upstream, preferred_element_type=jnp.float32)
    prob_grad = jnp.einsum("qhd,khd->hqk", upstream, value_part, preferred_element_type=jnp.float32)
    score_grad = soft_probs * (prob_grad - jnp.sum(prob_grad * soft_probs, axis=2, keepdims=True))
    score_grad = (score_grad * HEAD_DIM ** (-0.5)).astype(jnp.bfloat16)
    query_grad = jnp.einsum(
        "hqk,khd->qhd", score_grad, key_part, preferred_element_type=jnp.float32
    )
    key_grad = jnp.einsum(
        "hqk,qhd->khd", score_grad, query_part, preferred_element_type=jnp.float32
    )
    return jnp.concatenate(
        [
            query_grad.reshape(length, inner_width).astype(jnp.bfloat16),
            key_grad.reshape(length, inner_width).astype(jnp.bfloat16),
            value_grad.reshape(length, inner_width).astype(jnp.bfloat16),
        ],
        axis=1,
    )


def finish(mixed, kernel, segment):
    length = mixed.shape[0]
    tap_count = kernel.shape[0]
    half_span = (tap_count - 1) // 2
    signal = mixed.astype(jnp.float32)
    padded = jnp.pad(signal, ((half_span, half_span), (0, 0)))
    neighbours = jnp.pad(segment, (half_span, half_span), constant_values=-2)
    convolved = jnp.zeros_like(signal)
    for offset in range(tap_count):
        matching = (neighbours[offset : offset + length] == segment).astype(jnp.float32)
        convolved = (
            convolved + kernel[offset] * padded[offset : offset + length] * matching[:, None]
        )
    return signal + jax.nn.silu(convolved)


def body(projected, out_weight, kernel, cotangent, send_rows, compute_src, segment):
    row_count = projected.shape[0]
    present = send_rows >= 0
    outgoing = jnp.take(projected, jnp.maximum(send_rows, 0), axis=0)
    outgoing = jnp.where(present[:, None], outgoing, jnp.zeros_like(outgoing))
    incoming = lax.all_to_all(outgoing, DP, split_axis=0, concat_axis=0, tiled=True)
    filled = compute_src >= 0
    frames = jnp.take(incoming, jnp.maximum(compute_src, 0), axis=0)
    frames = jnp.where(filled[:, None], frames, jnp.zeros_like(frames))
    context, soft_probs, rounded = attend(frames, segment)
    columns = context
    mixed_sums = jnp.dot(
        columns,
        lax.all_gather(out_weight, FSDP, axis=0, tiled=True),
        preferred_element_type=jnp.float32,
    )
    mixed = mixed_sums.astype(jnp.bfloat16)
    result, pullback = jax.vjp(
        lambda signal, kernel_taps: finish(signal, kernel_taps, segment), mixed, kernel
    )
    mixed_grad, kernel_part = pullback(cotangent.astype(jnp.float32))
    columns = context
    weight_share = lax.psum_scatter(
        jnp.einsum("rc,rd->cd", columns, mixed_grad, preferred_element_type=jnp.float32).astype(
            jnp.bfloat16
        ),
        FSDP,
        scatter_dimension=0,
        tiled=True,
    ).astype(jnp.float32)
    context_grad = jnp.einsum(
        "rd,cd->rc",
        mixed_grad,
        lax.all_gather(out_weight, FSDP, axis=0, tiled=True),
        preferred_element_type=jnp.float32,
    ).astype(jnp.bfloat16)
    frame_grad = attend_back(frames, soft_probs, rounded, context_grad)
    slot_total = incoming.shape[0]
    back_index = jnp.where(filled, compute_src, slot_total)
    returning = jnp.zeros_like(incoming).at[back_index].set(frame_grad, mode="drop")
    arrived = lax.all_to_all(returning, DP, split_axis=0, concat_axis=0, tiled=True)
    source_index = jnp.where(present, send_rows, row_count)
    projected_grad = jnp.zeros_like(projected).at[source_index].set(arrived, mode="drop")
    scale_factor = (row_count * lax.axis_size(DP) * lax.axis_size(FSDP)) ** (-0.5)
    weight_share, arrived = lax.optimization_barrier((weight_share, arrived))
    kernel_piece = sum_rows(kernel_part, FSDP)
    owned_rows = weight_share.shape[0]
    both = jnp.concatenate([weight_share, kernel_piece], axis=0)
    piece = sum_rows(both, DP)
    both = gather_rows(piece, DP)[: both.shape[0]]
    weight_total = both[:owned_rows]
    kernel_total = gather_rows(both[owned_rows:], FSDP)[: kernel.shape[0]]

    return (
        result.astype(jnp.bfloat16),
        projected_grad,
        weight_total * scale_factor,
        kernel_total * scale_factor,
    )


def sum_rows(x, axis):
    count = lax.axis_size(axis)
    per = -(-x.shape[0] // count)
    padded = jnp.pad(x, ((0, count * per - x.shape[0]), (0, 0)))
    got = lax.all_to_all(padded.reshape(count, per, x.shape[1]), axis, split_axis=0, concat_axis=0, tiled=True)
    return jnp.sum(got, axis=0)


def gather_rows(piece, axis):
    count = lax.axis_size(axis)
    copies = jnp.broadcast_to(piece[None], (count, *piece.shape))
    got = lax.all_to_all(copies, axis, split_axis=0, concat_axis=0, tiled=True)
    return got.reshape(count * piece.shape[0], piece.shape[1])

def solution(mesh):
    dp_count, fsdp_count = mesh.devices.shape
    fine = Mesh(
        mesh.devices.reshape(dp_count // 4, 4, fsdp_count // 2, 2), ("dz", "dx", "fy", "fc")
    )
    placed = (
        P((*DP, *FSDP), None),
        P(FSDP, None),
        P(),
        P((*DP, *FSDP), None),
        P((*DP, *FSDP)),
        P((*DP, *FSDP)),
        P((*DP, *FSDP)),
    )
    return jax.shard_map(
        body,
        mesh=fine,
        in_specs=placed,
        out_specs=(P((*DP, *FSDP), None), P((*DP, *FSDP), None), P(FSDP, None), P()),
        check_vma=False,
    )
```

```python
import jax
import jax.numpy as jnp
from jax import lax
from jax.sharding import Mesh, PartitionSpec as P

DP = ("dz", "dx")
FSDP = ("fy", "fc")

HEADS = 8
HEAD_DIM = 96


def split_heads(frames):
    length = frames.shape[0]
    inner_width = HEADS * HEAD_DIM
    query_part = frames[:, :inner_width].reshape(length, HEADS, HEAD_DIM)
    key_part = frames[:, inner_width : 2 * inner_width].reshape(length, HEADS, HEAD_DIM)
    value_part = frames[:, 2 * inner_width :].reshape(length, HEADS, HEAD_DIM)
    return (query_part, key_part, value_part)


def attend(frames, segment):
    query_part, key_part, value_part = split_heads(frames)
    scores = jnp.einsum(
        "qhd,khd->hqk", query_part, key_part, preferred_element_type=jnp.float32
    ) * HEAD_DIM ** (-0.5)
    inside = segment[:, None] == segment[None, :]
    scores = jnp.where(inside[None], scores, -1e30)
    highest = jnp.max(scores, axis=2, keepdims=True)
    weights = jnp.exp(scores - highest)
    soft_probs = weights / jnp.sum(weights, axis=2, keepdims=True)
    rounded = soft_probs.astype(jnp.bfloat16)
    context = jnp.einsum("hqk,khd->qhd", rounded, value_part, preferred_element_type=jnp.float32)
    return (
        context.reshape(frames.shape[0], HEADS * HEAD_DIM).astype(jnp.bfloat16),
        soft_probs,
        rounded,
    )


def attend_back(frames, soft_probs, rounded, context_grad):
    query_part, key_part, value_part = split_heads(frames)
    length = frames.shape[0]
    inner_width = HEADS * HEAD_DIM
    upstream = context_grad.reshape(length, HEADS, HEAD_DIM)
    value_grad = jnp.einsum("hqk,qhd->khd", rounded, upstream, preferred_element_type=jnp.float32)
    prob_grad = jnp.einsum("qhd,khd->hqk", upstream, value_part, preferred_element_type=jnp.float32)
    score_grad = soft_probs * (prob_grad - jnp.sum(prob_grad * soft_probs, axis=2, keepdims=True))
    score_grad = (score_grad * HEAD_DIM ** (-0.5)).astype(jnp.bfloat16)
    query_grad = jnp.einsum(
        "hqk,khd->qhd", score_grad, key_part, preferred_element_type=jnp.float32
    )
    key_grad = jnp.einsum(
        "hqk,qhd->khd", score_grad, query_part, preferred_element_type=jnp.float32
    )
    return jnp.concatenate(
        [
            query_grad.reshape(length, inner_width).astype(jnp.bfloat16),
            key_grad.reshape(length, inner_width).astype(jnp.bfloat16),
            value_grad.reshape(length, inner_width).astype(jnp.bfloat16),
        ],
        axis=1,
    )


def finish(mixed, kernel, segment):
    length = mixed.shape[0]
    tap_count = kernel.shape[0]
    half_span = (tap_count - 1) // 2
    signal = mixed.astype(jnp.float32)
    padded = jnp.pad(signal, ((half_span, half_span), (0, 0)))
    neighbours = jnp.pad(segment, (half_span, half_span), constant_values=-2)
    convolved = jnp.zeros_like(signal)
    for offset in range(tap_count):
        matching = (neighbours[offset : offset + length] == segment).astype(jnp.float32)
        convolved = (
            convolved + kernel[offset] * padded[offset : offset + length] * matching[:, None]
        )
    return signal + jax.nn.silu(convolved)


def body(projected, out_weight, kernel, cotangent, send_rows, compute_src, segment):
    row_count = projected.shape[0]
    present = send_rows >= 0
    outgoing = jnp.take(projected, jnp.maximum(send_rows, 0), axis=0)
    outgoing = jnp.where(present[:, None], outgoing, jnp.zeros_like(outgoing))
    incoming = lax.all_to_all(outgoing, DP, split_axis=0, concat_axis=0, tiled=True)
    filled = compute_src >= 0
    frames = jnp.take(incoming, jnp.maximum(compute_src, 0), axis=0)
    frames = jnp.where(filled[:, None], frames, jnp.zeros_like(frames))
    context, soft_probs, rounded = attend(frames, segment)
    columns = context
    mixed_sums = jnp.dot(
        columns,
        lax.all_gather(out_weight, FSDP, axis=0, tiled=True),
        preferred_element_type=jnp.float32,
    )
    mixed = mixed_sums.astype(jnp.bfloat16)
    result, pullback = jax.vjp(
        lambda signal, kernel_taps: finish(signal, kernel_taps, segment), mixed, kernel
    )
    mixed_grad, kernel_part = pullback(cotangent.astype(jnp.float32))
    columns = context
    weight_share = lax.psum_scatter(
        jnp.einsum("rc,rd->cd", columns, mixed_grad, preferred_element_type=jnp.float32).astype(
            jnp.bfloat16
        ),
        FSDP,
        scatter_dimension=0,
        tiled=True,
    ).astype(jnp.float32)
    context_grad = jnp.einsum(
        "rd,cd->rc",
        mixed_grad,
        lax.all_gather(out_weight, FSDP, axis=0, tiled=True),
        preferred_element_type=jnp.float32,
    ).astype(jnp.bfloat16)
    frame_grad = attend_back(frames, soft_probs, rounded, context_grad)
    slot_total = incoming.shape[0]
    back_index = jnp.where(filled, compute_src, slot_total)
    returning = jnp.zeros_like(incoming).at[back_index].set(frame_grad, mode="drop")
    arrived = lax.all_to_all(returning, DP, split_axis=0, concat_axis=0, tiled=True)
    source_index = jnp.where(present, send_rows, row_count)
    projected_grad = jnp.zeros_like(projected).at[source_index].set(arrived, mode="drop")
    scale_factor = (row_count * lax.axis_size(DP) * lax.axis_size(FSDP)) ** (-0.5)
    weight_share, arrived = lax.optimization_barrier((weight_share, arrived))
    kernel_piece = sum_rows(kernel_part, FSDP)
    owned_rows = weight_share.shape[0]
    both = jnp.concatenate([weight_share, kernel_piece], axis=0)
    piece = sum_rows(both, DP)
    both = gather_rows(piece, DP)[: both.shape[0]]
    weight_total = both[:owned_rows]
    kernel_total = gather_rows(gather_rows(both[owned_rows:], "fc"), "fy")[: kernel.shape[0]]

    return (
        result.astype(jnp.bfloat16),
        projected_grad,
        weight_total * scale_factor,
        kernel_total * scale_factor,
    )


def sum_rows(x, axis):
    count = lax.axis_size(axis)
    per = -(-x.shape[0] // count)
    padded = jnp.pad(x, ((0, count * per - x.shape[0]), (0, 0)))
    got = lax.all_to_all(padded.reshape(count, per, x.shape[1]), axis, split_axis=0, concat_axis=0, tiled=True)
    return jnp.sum(got, axis=0)


def gather_rows(piece, axis):
    count = lax.axis_size(axis)
    copies = jnp.broadcast_to(piece[None], (count, *piece.shape))
    got = lax.all_to_all(copies, axis, split_axis=0, concat_axis=0, tiled=True)
    return got.reshape(count * piece.shape[0], piece.shape[1])

def solution(mesh):
    dp_count, fsdp_count = mesh.devices.shape
    fine = Mesh(
        mesh.devices.reshape(dp_count // 4, 4, fsdp_count // 2, 2), ("dz", "dx", "fy", "fc")
    )
    placed = (
        P((*DP, *FSDP), None),
        P(FSDP, None),
        P(),
        P((*DP, *FSDP), None),
        P((*DP, *FSDP)),
        P((*DP, *FSDP)),
        P((*DP, *FSDP)),
    )
    return jax.shard_map(
        body,
        mesh=fine,
        in_specs=placed,
        out_specs=(P((*DP, *FSDP), None), P((*DP, *FSDP), None), P(FSDP, None), P()),
        check_vma=False,
    )
```
